512 devices in a mesh: dp: 64 (over z, x), pair: 8 (over y, core).
Axes of the slice: x: 4, y: 4, z: 16, core: 2. Of those that a mesh axis runs over, the one named last changes fastest.
Arguments:
- embedding: bfloat16 [65536, 1024], P(('dp', 'pair')), may hold values from -32 to 32
- labels: int32 [65536], P(('dp', 'pair')), may hold values from 0 to 127, as said below
- order_ids: int32 [65536], P(('dp', 'pair')), may hold values from 0 to 65535, each once
Outputs:
- best_similarity: float32 [65536], P(('dp', 'pair'))
The draws below stay inside these ranges and needn't reach their ends.
Inputs may be any that keep to these rules, and one draw needn't show every extreme that they name: `labels`: clusters 2 * g to 2 * g + 1 form owner group g. Among the 128 rows of one device (aligned blocks of the whole array) at most 4 name clusters of any one group, and in every draw some group gets exactly 4 rows from every device.
All inputs are finite; a program needn't handle non-finite values.
Results may differ from the reference program's by a relative error of at most 0.00049.
Values may be sent and summed in bfloat16 or wider, within the bound.
No kernel may reach another device: no remote copies, remote signals or barrier semaphores. Data moves between devices by JAX's collectives and lax.ppermute only.
A program may use at most 64 MiB of HBM per device.

```python
import math
import jax
import jax.numpy as jnp
from jax import lax

D = 1024
ROWS_DEV = 128
CL_OWN = 2
CAP = 4
ROWS = 65536
N_DP = 64
N_PAIR = 8


def route_layout(key):
    base_key = jax.random.fold_in(key, 17)
    key_list = jax.random.split(base_key, 4)
    hot_group = jax.random.randint(key_list[0], (), 0, N_DP).astype(jnp.int32)
    others = (N_DP - 1) * CAP

    def one_block(block_key):
        pick_key, shuffle_key, choose_key = jax.random.split(block_key, 3)
        tokens = jax.random.permutation(pick_key, others)[:ROWS_DEV - CAP].astype(jnp.int32)
        group_ids = tokens // CAP
        group_ids = group_ids + (group_ids >= hot_group).astype(jnp.int32)
        owners = jnp.concatenate([jnp.zeros((CAP,), jnp.int32) + hot_group, group_ids])
        owners = jax.random.permutation(shuffle_key, owners)
        within = jax.random.randint(choose_key, (ROWS_DEV,), 0, CL_OWN).astype(jnp.int32)
        return owners * CL_OWN + within
    labels = jax.vmap(one_block)(jax.random.split(key_list[1], N_DP * N_PAIR)).reshape(ROWS)
    families = max(ROWS_DEV * N_PAIR // (4 * CL_OWN), 1)
    family_ids = labels * families + jax.random.randint(key_list[2], (ROWS,), 0, families).astype(jnp.int32)
    return (labels, family_ids, key_list[3])


def draw_labels(key, part):
    return route_layout(key)[0]


def draw_embedding(key, part):
    labels, family_ids, float_key = route_layout(key)
    center_key, family_key, noise_key, spread_key = jax.random.split(float_key, 4)

    def center_vector(number_id):
        return jax.random.normal(jax.random.fold_in(center_key, number_id), (D,), jnp.float32)

    def family_vector(number_id):
        return jax.random.normal(jax.random.fold_in(family_key, number_id), (D,), jnp.float32)
    center = jax.vmap(center_vector)(labels)
    family_part = jax.vmap(family_vector)(family_ids)
    noise_part = jax.random.normal(noise_key, (ROWS, D), jnp.float32)
    spread = jnp.exp(jax.random.uniform(spread_key, (ROWS, 1), jnp.float32, math.log(0.25), math.log(1.5)))
    drawn = 0.7 * center + family_part + spread * noise_part
    return jnp.clip(drawn, -32.0, 32.0).astype(jnp.bfloat16)


def setup_inputs(seed: int = 0) -> dict:
    splits = jax.random.split(jax.random.key(seed), 4)
    return {
        "embedding": draw_embedding(jax.random.fold_in(splits[3], 71), 0),
        "labels": draw_labels(jax.random.fold_in(splits[3], 71), 0),
        "order_ids": jax.random.permutation(splits[2], ROWS).astype(jnp.int32),
    }


def reference(embedding, labels, order_ids):
    values = embedding.astype(jnp.float32)
    squares = lax.optimization_barrier(jnp.sum(values * values, axis=1, keepdims=True))
    shifted = squares + 1e-06
    unit_rows = (values * lax.rsqrt(shifted)).astype(jnp.bfloat16)
    sort_keys = labels.astype(jnp.int32) * ROWS + order_ids.astype(jnp.int32)
    sorted_at = jnp.argsort(sort_keys).astype(jnp.int32)
    sorted_rows = unit_rows[sorted_at].astype(jnp.float32)
    sorted_labels = labels[sorted_at].astype(jnp.int32)
    position = jnp.arange(ROWS, dtype=jnp.int32)
    opening = (position == 0) | (sorted_labels != jnp.roll(sorted_labels, 1))
    cluster_start = lax.cummax(jnp.where(opening, position, 0).astype(jnp.int32), axis=0)
    tile_rows = 256

    def one_block(block_index):
        query_start = (block_index * tile_rows).astype(jnp.int32)
        queries = lax.dynamic_slice_in_dim(sorted_rows, query_start, tile_rows, 0)
        query_labels = lax.dynamic_slice_in_dim(sorted_labels, query_start, tile_rows, 0)
        query_pos = query_start + jnp.arange(tile_rows, dtype=jnp.int32)

        def add_tile(tile_index, best_seen):
            key_start = (tile_index * tile_rows).astype(jnp.int32)
            key_rows = lax.dynamic_slice_in_dim(sorted_rows, key_start, tile_rows, 0)
            key_labels = lax.dynamic_slice_in_dim(sorted_labels, key_start, tile_rows, 0)
            key_pos = key_start + jnp.arange(tile_rows, dtype=jnp.int32)
            scores = jnp.dot(queries, key_rows.T, precision=lax.Precision.HIGHEST)
            usable = (key_labels[None, :] == query_labels[:, None]) & (key_pos[None, :] < query_pos[:, None])
            return jnp.maximum(best_seen, lax.optimization_barrier(jnp.max(jnp.where(usable, scores, -1.0), axis=1)))
        first_tile = (cluster_start[query_start] // tile_rows).astype(jnp.int32)
        return lax.fori_loop(first_tile, block_index + 1, add_tile, jnp.full((tile_rows,), -1.0, jnp.float32))
    best_sorted = lax.map(one_block, jnp.arange(ROWS // tile_rows, dtype=jnp.int32)).reshape(ROWS)
    return jnp.zeros((ROWS,), jnp.float32).at[sorted_at].set(best_sorted)
```

```python
import jax
import jax.numpy as jnp
from jax import lax
from jax.sharding import PartitionSpec as P

CL_OWN = 2
META = 128


def tile_best(own_rows, own_key, other_rows, other_key, rows_total):
    scores = jnp.dot(own_rows, other_rows.T, preferred_element_type=jnp.float32)
    same_cluster = (other_key[None, :] // rows_total) == (own_key[:, None] // rows_total)
    earlier = same_cluster & (other_key[None, :] < own_key[:, None])
    return jnp.max(jnp.where(earlier, scores, -1.0), axis=1)


def slot_keys(rows, width, rows_total):
    meta = rows[:, width : width + 3].astype(jnp.int32)
    return meta[:, 0] * rows_total + meta[:, 1] * 256 + meta[:, 2]


def on_device(embedding, labels, order_ids):
    groups = lax.axis_size("dp")
    pairs = lax.axis_size("pair")
    rows_here, width = embedding.shape
    rows_total = rows_here * groups * pairs
    capacity = 2 * rows_here // groups
    slot_count = groups * capacity
    values = embedding.astype(jnp.float32)
    squares = jnp.sum(values * values, axis=1, keepdims=True)
    shifted = squares + 1e-06
    unit_rows = (values * lax.rsqrt(shifted)).astype(jnp.bfloat16)
    owner_group = labels // CL_OWN
    onehot = (owner_group[:, None] == jnp.arange(groups, dtype=jnp.int32)[None, :]).astype(
        jnp.int32
    )
    before = jnp.cumsum(onehot, axis=0) - onehot
    slot_index = owner_group * capacity + jnp.sum(before * onehot, axis=1)
    meta = jnp.stack([labels + 1, order_ids // 256, order_ids % 256], axis=1).astype(jnp.bfloat16)
    meta = jnp.pad(meta, ((0, 0), (0, META - 3)))
    packed = jnp.concatenate([unit_rows, meta], axis=1)
    send_rows = jnp.zeros((slot_count, width + META), jnp.bfloat16).at[slot_index].set(packed)
    got_rows = lax.all_to_all(
        send_rows.reshape(groups, capacity, -1), "dp", split_axis=0, concat_axis=0, tiled=True
    ).reshape(slot_count, -1)
    piece_rows = lax.all_gather(got_rows, "pair", axis=0, tiled=True)
    got_key = slot_keys(got_rows, width, rows_total)
    piece_key = slot_keys(piece_rows, width, rows_total)
    column = lax.broadcasted_iota(jnp.int32, got_rows.shape, 1)
    query_rows = jnp.where(column < width, got_rows, jnp.zeros_like(got_rows))
    best_seen = jnp.full((slot_count,), -1.0, jnp.float32)
    piece_count = piece_rows.shape[0]
    for offset in range(0, piece_count, 512):
        width_now = min(512, piece_count - offset)
        found = tile_best(
            query_rows,
            got_key,
            piece_rows[offset : offset + width_now],
            piece_key[offset : offset + width_now],
            rows_total,
        )
        best_seen = jnp.maximum(best_seen, found)
    answered = lax.all_to_all(
        best_seen.reshape(groups, capacity), "dp", split_axis=0, concat_axis=0, tiled=True
    )
    return answered.reshape(slot_count)[slot_index]


def solution(mesh):
    in_specs = (P(("dp", "pair"), None), P(("dp", "pair")), P(("dp", "pair")))
    out_specs = P(("dp", "pair"))
    return jax.shard_map(
        on_device, mesh=mesh, in_specs=in_specs, out_specs=out_specs, check_vma=False
    )
```

```python
import jax
import jax.numpy as jnp
from jax import lax
from jax.sharding import PartitionSpec as P

CL_OWN = 2
META = 128
PUBLISH_ROWS = 32


def tile_best(own_rows, own_key, other_rows, other_key, rows_total):
    scores = jnp.dot(own_rows, other_rows.T, preferred_element_type=jnp.float32)
    same_cluster = (other_key[None, :] // rows_total) == (own_key[:, None] // rows_total)
    earlier = same_cluster & (other_key[None, :] < own_key[:, None])
    return jnp.max(jnp.where(earlier, scores, -1.0), axis=1)


def slot_keys(rows, width, rows_total):
    meta = rows[:, width : width + 3].astype(jnp.int32)
    return meta[:, 0] * rows_total + meta[:, 1] * 256 + meta[:, 2]


def on_device(embedding, labels, order_ids):
    groups = lax.axis_size("dp")
    pairs = lax.axis_size("pair")
    rows_here, width = embedding.shape
    rows_total = rows_here * groups * pairs
    capacity = 2 * rows_here // groups
    slot_count = groups * capacity
    values = embedding.astype(jnp.float32)
    squares = jnp.sum(values * values, axis=1, keepdims=True)
    shifted = squares + 1e-06
    unit_rows = (values * lax.rsqrt(shifted)).astype(jnp.bfloat16)
    owner_group = labels // CL_OWN
    onehot = (owner_group[:, None] == jnp.arange(groups, dtype=jnp.int32)[None, :]).astype(
        jnp.int32
    )
    before = jnp.cumsum(onehot, axis=0) - onehot
    slot_index = owner_group * capacity + jnp.sum(before * onehot, axis=1)
    meta = jnp.stack([labels + 1, order_ids // 256, order_ids % 256], axis=1).astype(jnp.bfloat16)
    meta = jnp.pad(meta, ((0, 0), (0, META - 3)))
    packed = jnp.concatenate([unit_rows, meta], axis=1)
    send_rows = jnp.zeros((slot_count, width + META), jnp.bfloat16).at[slot_index].set(packed)
    got_rows = lax.all_to_all(
        send_rows.reshape(groups, capacity, -1), "dp", split_axis=0, concat_axis=0, tiled=True
    ).reshape(slot_count, -1)
    piece_rows = lax.all_gather(got_rows, "pair", axis=0, tiled=True)
    got_key = slot_keys(got_rows, width, rows_total)
    piece_key = slot_keys(piece_rows, width, rows_total)
    column = lax.broadcasted_iota(jnp.int32, got_rows.shape, 1)
    query_rows = jnp.where(column < width, got_rows, jnp.zeros_like(got_rows))
    best_seen = jnp.full((slot_count,), -1.0, jnp.float32)
    piece_count = piece_rows.shape[0]
    for offset in range(0, piece_count, 512):
        width_now = min(512, piece_count - offset)
        found = tile_best(
            query_rows,
            got_key,
            piece_rows[offset : offset + width_now],
            piece_key[offset : offset + width_now],
            rows_total,
        )
        best_seen = jnp.maximum(best_seen, found)
    publish = jnp.zeros((PUBLISH_ROWS * 128,), jnp.float32).at[:slot_count].set(best_seen)
    published = lax.all_gather(publish.reshape(PUBLISH_ROWS, 128), "dp", axis=0, tiled=False)
    me = lax.axis_index("dp")
    answered = lax.dynamic_slice_in_dim(
        published.reshape(groups, PUBLISH_ROWS * 128), me * capacity, capacity, axis=1
    )
    return answered.reshape(slot_count)[slot_index]


def solution(mesh):
    in_specs = (P(("dp", "pair"), None), P(("dp", "pair")), P(("dp", "pair")))
    out_specs = P(("dp", "pair"))
    return jax.shard_map(
        on_device, mesh=mesh, in_specs=in_specs, out_specs=out_specs, check_vma=False
    )
```

```python
import jax
import jax.numpy as jnp
from jax import lax
from jax.sharding import Mesh, PartitionSpec as P

CL_OWN = 2
META = 128


def tile_best(own_rows, own_key, other_rows, other_key, rows_total):
    scores = jnp.dot(own_rows, other_rows.T, preferred_element_type=jnp.float32)
    same_cluster = (other_key[None, :] // rows_total) == (own_key[:, None] // rows_total)
    earlier = same_cluster & (other_key[None, :] < own_key[:, None])
    return jnp.max(jnp.where(earlier, scores, -1.0), axis=1)


def slot_keys(rows, width, rows_total):
    meta = rows[:, width : width + 3].astype(jnp.int32)
    return meta[:, 0] * rows_total + meta[:, 1] * 256 + meta[:, 2]


def on_device(embedding, labels, order_ids):
    groups = lax.axis_size("dp")
    pairs = lax.axis_size("y") * lax.axis_size("core")
    rows_here, width = embedding.shape
    rows_total = rows_here * groups * pairs
    capacity = 2 * rows_here // groups
    slot_count = groups * capacity
    values = embedding.astype(jnp.float32)
    squares = jnp.sum(values * values, axis=1, keepdims=True)
    shifted = squares + 1e-06
    unit_rows = (values * lax.rsqrt(shifted)).astype(jnp.bfloat16)
    owner_group = labels // CL_OWN
    onehot = (owner_group[:, None] == jnp.arange(groups, dtype=jnp.int32)[None, :]).astype(
        jnp.int32
    )
    before = jnp.cumsum(onehot, axis=0) - onehot
    slot_index = owner_group * capacity + jnp.sum(before * onehot, axis=1)
    meta = jnp.stack([labels + 1, order_ids // 256, order_ids % 256], axis=1).astype(jnp.bfloat16)
    meta = jnp.pad(meta, ((0, 0), (0, META - 3)))
    packed = jnp.concatenate([unit_rows, meta], axis=1)
    send_rows = jnp.zeros((slot_count, width + META), jnp.bfloat16).at[slot_index].set(packed)
    got_rows = lax.all_to_all(
        send_rows.reshape(groups, capacity, -1), "dp", split_axis=0, concat_axis=0, tiled=True
    ).reshape(slot_count, -1)
    piece_rows = lax.all_gather(got_rows, "y", axis=0, tiled=True)
    piece_rows = lax.all_gather(piece_rows, "core", axis=0, tiled=True)
    got_key = slot_keys(got_rows, width, rows_total)
    piece_key = slot_keys(piece_rows, width, rows_total)
    column = lax.broadcasted_iota(jnp.int32, got_rows.shape, 1)
    query_rows = jnp.where(column < width, got_rows, jnp.zeros_like(got_rows))
    best_seen = jnp.full((slot_count,), -1.0, jnp.float32)
    piece_count = piece_rows.shape[0]
    for offset in range(0, piece_count, 512):
        width_now = min(512, piece_count - offset)
        found = tile_best(
            query_rows,
            got_key,
            piece_rows[offset : offset + width_now],
            piece_key[offset : offset + width_now],
            rows_total,
        )
        best_seen = jnp.maximum(best_seen, found)
    answered = lax.all_to_all(
        best_seen.reshape(groups, capacity), "dp", split_axis=0, concat_axis=0, tiled=True
    )
    return answered.reshape(slot_count)[slot_index]


def solution(mesh):
    cores = 2
    split = Mesh(
        mesh.devices.reshape(mesh.shape["dp"], mesh.shape["pair"] // cores, cores),
        ("dp", "y", "core"),
    )
    rows = ("dp", "y", "core")
    in_specs = (P(rows, None), P(rows), P(rows))
    out_specs = P(rows)
    return jax.shard_map(
        on_device, mesh=split, in_specs=in_specs, out_specs=out_specs, check_vma=False
    )
```

```python
import jax
import jax.numpy as jnp
from jax import lax
from jax.sharding import PartitionSpec as P

CL_OWN = 2
META = 128


def slot_best(query_rows, query_key, key_rows, key_key, rows_total):
    scores = jnp.dot(query_rows, key_rows.T, preferred_element_type=jnp.float32)
    same_cluster = (key_key[None, :] // rows_total) == (query_key[:, None] // rows_total)
    earlier = same_cluster & (key_key[None, :] < query_key[:, None])
    return jnp.max(jnp.where(earlier, scores, -1.0), axis=1)


def chunk_keys(chunks, capacity, width, rows_total):
    start = capacity * width
    meta = chunks[:, start : start + 3 * capacity].astype(jnp.int32)
    meta = meta.reshape(chunks.shape[0], capacity, 3)
    return meta[:, :, 0] * rows_total + meta[:, :, 1] * 256 + meta[:, :, 2]


def on_device(embedding, labels, order_ids):
    groups = lax.axis_size("dp")
    pairs = lax.axis_size("pair")
    rows_here, width = embedding.shape
    rows_total = rows_here * groups * pairs
    capacity = 2 * rows_here // groups
    slot_count = groups * capacity
    values = embedding.astype(jnp.float32)
    squares = jnp.sum(values * values, axis=1, keepdims=True)
    shifted = squares + 1e-06
    unit_rows = (values * lax.rsqrt(shifted)).astype(jnp.bfloat16)
    owner_group = labels // CL_OWN
    onehot = (owner_group[:, None] == jnp.arange(groups, dtype=jnp.int32)[None, :]).astype(
        jnp.int32
    )
    before = jnp.cumsum(onehot, axis=0) - onehot
    rank = jnp.sum(before * onehot, axis=1)
    slot_index = owner_group * capacity + rank
    meta = jnp.stack([labels + 1, order_ids // 256, order_ids % 256], axis=1).astype(jnp.bfloat16)
    pieces = []
    meta_pieces = []
    for k in range(capacity):
        pick = ((owner_group[None, :] == jnp.arange(groups, dtype=jnp.int32)[:, None])
                & (rank[None, :] == k)).astype(jnp.bfloat16)
        pieces.append(jnp.dot(pick, unit_rows, preferred_element_type=jnp.float32))
        meta_pieces.append(jnp.dot(pick, meta, preferred_element_type=jnp.float32))
    meta_block = jnp.concatenate(meta_pieces, axis=1)
    meta_block = jnp.pad(meta_block, ((0, 0), (0, META - meta_block.shape[1])))
    send = jnp.concatenate(pieces + [meta_block], axis=1).astype(jnp.bfloat16)
    got = lax.all_to_all(send, "dp", split_axis=0, concat_axis=0, tiled=True)
    piece = lax.all_gather(got, "pair", axis=0, tiled=True)
    got_key = chunk_keys(got, capacity, width, rows_total).reshape(slot_count)
    piece_key = chunk_keys(piece, capacity, width, rows_total)
    query_rows = got[:, : capacity * width].reshape(slot_count, width)
    best_seen = jnp.full((slot_count,), -1.0, jnp.float32)
    for k in range(capacity):
        found = slot_best(
            query_rows,
            got_key,
            piece[:, k * width : (k + 1) * width],
            piece_key[:, k],
            rows_total,
        )
        best_seen = jnp.maximum(best_seen, found)
    answered = lax.all_to_all(best_seen, "dp", split_axis=0, concat_axis=0, tiled=True)
    mine = slot_index[:, None] == jnp.arange(slot_count, dtype=jnp.int32)[None, :]
    return jnp.max(jnp.where(mine, answered[None, :], -jnp.inf), axis=1)


def solution(mesh):
    in_specs = (P(("dp", "pair"), None), P(("dp", "pair")), P(("dp", "pair")))
    out_specs = P(("dp", "pair"))
    return jax.shard_map(
        on_device, mesh=mesh, in_specs=in_specs, out_specs=out_specs, check_vma=False
    )
```

```python
import jax
import jax.numpy as jnp
from jax import lax
from jax.sharding import PartitionSpec as P

CL_OWN = 2
META = 128
KEY_TILE = 2048


def tile_best(own_rows, own_key, other_rows, other_key, rows_total):
    scores = jnp.dot(own_rows, other_rows.T, preferred_element_type=jnp.float32)
    same_cluster = (other_key[None, :] // rows_total) == (own_key[:, None] // rows_total)
    earlier = same_cluster & (other_key[None, :] < own_key[:, None])
    return jnp.max(jnp.where(earlier, scores, -1.0), axis=1)


def slot_keys(rows, width, rows_total):
    meta = rows[:, width : width + 3].astype(jnp.int32)
    return meta[:, 0] * rows_total + meta[:, 1] * 256 + meta[:, 2]


def on_device(embedding, labels, order_ids):
    groups = lax.axis_size("dp")
    pairs = lax.axis_size("pair")
    rows_here, width = embedding.shape
    rows_total = rows_here * groups * pairs
    capacity = 2 * rows_here // groups
    slot_count = groups * capacity
    values = embedding.astype(jnp.float32)
    squares = jnp.sum(values * values, axis=1, keepdims=True)
    shifted = squares + 1e-06
    unit_rows = (values * lax.rsqrt(shifted)).astype(jnp.bfloat16)
    owner_group = labels // CL_OWN
    onehot = (owner_group[:, None] == jnp.arange(groups, dtype=jnp.int32)[None, :]).astype(
        jnp.int32
    )
    before = jnp.cumsum(onehot, axis=0) - onehot
    slot_index = owner_group * capacity + jnp.sum(before * onehot, axis=1)
    meta = jnp.stack([labels + 1, order_ids // 256, order_ids % 256], axis=1).astype(jnp.bfloat16)
    meta = jnp.pad(meta, ((0, 0), (0, META - 3)))
    packed = jnp.concatenate([unit_rows, meta], axis=1)
    send_rows = jnp.zeros((slot_count, width + META), jnp.bfloat16).at[slot_index].set(packed)
    got_rows = lax.all_to_all(
        send_rows.reshape(groups, capacity, -1), "dp", split_axis=0, concat_axis=0, tiled=True
    ).reshape(slot_count, -1)
    piece_rows = lax.all_gather(got_rows, "pair", axis=0, tiled=True)
    got_key = slot_keys(got_rows, width, rows_total)
    piece_key = slot_keys(piece_rows, width, rows_total)
    column = lax.broadcasted_iota(jnp.int32, got_rows.shape, 1)
    query_rows = jnp.where(column < width, got_rows, jnp.zeros_like(got_rows))
    best_seen = jnp.full((slot_count,), -1.0, jnp.float32)
    piece_count = piece_rows.shape[0]
    for offset in range(0, piece_count, KEY_TILE):
        width_now = min(KEY_TILE, piece_count - offset)
        found = tile_best(
            query_rows,
            got_key,
            piece_rows[offset : offset + width_now],
            piece_key[offset : offset + width_now],
            rows_total,
        )
        best_seen = jnp.maximum(best_seen, found)
    answered = lax.all_to_all(
        best_seen.reshape(groups, capacity), "dp", split_axis=0, concat_axis=0, tiled=True
    )
    mine = slot_index[:, None] == jnp.arange(slot_count, dtype=jnp.int32)[None, :]
    return jnp.max(jnp.where(mine, answered.reshape(1, slot_count), -jnp.inf), axis=1)


def solution(mesh):
    in_specs = (P(("dp", "pair"), None), P(("dp", "pair")), P(("dp", "pair")))
    out_specs = P(("dp", "pair"))
    return jax.shard_map(
        on_device, mesh=mesh, in_specs=in_specs, out_specs=out_specs, check_vma=False
    )
```

```python
import jax
import jax.numpy as jnp
from jax import lax
from jax.sharding import PartitionSpec as P

CL_OWN = 2
META = 128


def tile_best(own_rows, own_key, other_rows, other_key, rows_total):
    scores = jnp.dot(own_rows, other_rows.T, preferred_element_type=jnp.float32)
    same_cluster = (other_key[None, :] // rows_total) == (own_key[:, None] // rows_total)
    earlier = same_cluster & (other_key[None, :] < own_key[:, None])
    return jnp.max(jnp.where(earlier, scores, -1.0), axis=1)


def slot_keys(rows, width, rows_total):
    meta = rows[:, width : width + 3].astype(jnp.int32)
    return meta[:, 0] * rows_total + meta[:, 1] * 256 + meta[:, 2]


def pair_blocks(block, pairs):
    chips = pairs // 2
    if pairs % 2 or chips != 4:
        gathered = lax.all_gather(block, "pair", axis=0, tiled=True)
        return jnp.split(gathered, pairs, axis=0)

    def at(y, c):
        return (y % chips) * 2 + c

    def perm(to):
        return [(p, to(p // 2, p % 2)) for p in range(pairs)]

    swap = perm(lambda y, c: at(y, 1 - c))
    up = perm(lambda y, c: at(y + 1, c))
    down = perm(lambda y, c: at(y - 1, c))
    cross = perm(lambda y, c: at(y - 1, 1 - c))
    sibling = lax.ppermute(block, "pair", swap)
    from_below = lax.ppermute(block, "pair", up)
    from_above = lax.ppermute(block, "pair", down)
    two_below = lax.ppermute(from_below, "pair", up)
    two_above = lax.ppermute(from_above, "pair", cross)
    sibling_below = lax.ppermute(from_below, "pair", swap)
    sibling_above = lax.ppermute(from_above, "pair", swap)
    return [block, sibling, from_below, from_above, two_below, two_above, sibling_below,
            sibling_above]


def on_device(embedding, labels, order_ids):
    groups = lax.axis_size("dp")
    pairs = lax.axis_size("pair")
    rows_here, width = embedding.shape
    rows_total = rows_here * groups * pairs
    capacity = 2 * rows_here // groups
    slot_count = groups * capacity
    values = embedding.astype(jnp.float32)
    squares = jnp.sum(values * values, axis=1, keepdims=True)
    shifted = squares + 1e-06
    unit_rows = (values * lax.rsqrt(shifted)).astype(jnp.bfloat16)
    owner_group = labels // CL_OWN
    onehot = (owner_group[:, None] == jnp.arange(groups, dtype=jnp.int32)[None, :]).astype(
        jnp.int32
    )
    before = jnp.cumsum(onehot, axis=0) - onehot
    slot_index = owner_group * capacity + jnp.sum(before * onehot, axis=1)
    meta = jnp.stack([labels + 1, order_ids // 256, order_ids % 256], axis=1).astype(jnp.bfloat16)
    meta = jnp.pad(meta, ((0, 0), (0, META - 3)))
    packed = jnp.concatenate([unit_rows, meta], axis=1)
    send_rows = jnp.zeros((slot_count, width + META), jnp.bfloat16).at[slot_index].set(packed)
    got_rows = lax.all_to_all(
        send_rows.reshape(groups, capacity, -1), "dp", split_axis=0, concat_axis=0, tiled=True
    ).reshape(slot_count, -1)
    blocks = pair_blocks(got_rows, pairs)
    got_key = slot_keys(got_rows, width, rows_total)
    column = lax.broadcasted_iota(jnp.int32, got_rows.shape, 1)
    query_rows = jnp.where(column < width, got_rows, jnp.zeros_like(got_rows))
    best_seen = jnp.full((slot_count,), -1.0, jnp.float32)
    for block in blocks:
        found = tile_best(
            query_rows, got_key, block, slot_keys(block, width, rows_total), rows_total
        )
        best_seen = jnp.maximum(best_seen, found)
    answered = lax.all_to_all(
        best_seen.reshape(groups, capacity), "dp", split_axis=0, concat_axis=0, tiled=True
    )
    mine = slot_index[:, None] == jnp.arange(slot_count, dtype=jnp.int32)[None, :]
    return jnp.max(jnp.where(mine, answered.reshape(1, slot_count), -jnp.inf), axis=1)


def solution(mesh):
    in_specs = (P(("dp", "pair"), None), P(("dp", "pair")), P(("dp", "pair")))
    out_specs = P(("dp", "pair"))
    return jax.shard_map(
        on_device, mesh=mesh, in_specs=in_specs, out_specs=out_specs, check_vma=False
    )
```

```python
import jax
import jax.numpy as jnp
from jax import lax
from jax.sharding import PartitionSpec as P

CL_OWN = 2
META = 128


def tile_best(own_rows, own_key, other_rows, other_key, rows_total):
    scores = jnp.dot(own_rows, other_rows.T, preferred_element_type=jnp.float32)
    same_cluster = (other_key[None, :] // rows_total) == (own_key[:, None] // rows_total)
    earlier = same_cluster & (other_key[None, :] < own_key[:, None])
    return jnp.max(jnp.where(earlier, scores, -1.0), axis=1)


def slot_keys(rows, width, rows_total):
    meta = rows[:, width : width + 3].astype(jnp.int32)
    return meta[:, 0] * rows_total + meta[:, 1] * 256 + meta[:, 2]


def pair_blocks(block, pairs):
    chips = pairs // 2
    if pairs % 2 or chips != 4:
        gathered = lax.all_gather(block, "pair", axis=0, tiled=True)
        return jnp.split(gathered, pairs, axis=0)

    def at(y, c):
        return (y % chips) * 2 + c

    def perm(to):
        return [(p, to(p // 2, p % 2)) for p in range(pairs)]

    swap = perm(lambda y, c: at(y, 1 - c))
    up = perm(lambda y, c: at(y + 1, c))
    down = perm(lambda y, c: at(y - 1, c))
    cross = perm(lambda y, c: at(y - 1, 1 - c))
    sibling = lax.ppermute(block, "pair", swap)
    from_below = lax.ppermute(block, "pair", up)
    from_above = lax.ppermute(block, "pair", down)
    two_below = lax.ppermute(from_below, "pair", up)
    two_above = lax.ppermute(from_above, "pair", cross)
    rows = block.shape[0]
    siblings = lax.ppermute(jnp.concatenate([from_below, from_above]), "pair", swap)
    return [block, sibling, from_below, from_above, two_below, two_above, siblings[:rows],
            siblings[rows:]]


def on_device(embedding, labels, order_ids):
    groups = lax.axis_size("dp")
    pairs = lax.axis_size("pair")
    rows_here, width = embedding.shape
    rows_total = rows_here * groups * pairs
    capacity = 2 * rows_here // groups
    slot_count = groups * capacity
    values = embedding.astype(jnp.float32)
    squares = jnp.sum(values * values, axis=1, keepdims=True)
    shifted = squares + 1e-06
    unit_rows = (values * lax.rsqrt(shifted)).astype(jnp.bfloat16)
    owner_group = labels // CL_OWN
    onehot = (owner_group[:, None] == jnp.arange(groups, dtype=jnp.int32)[None, :]).astype(
        jnp.int32
    )
    before = jnp.cumsum(onehot, axis=0) - onehot
    slot_index = owner_group * capacity + jnp.sum(before * onehot, axis=1)
    meta = jnp.stack([labels + 1, order_ids // 256, order_ids % 256], axis=1).astype(jnp.bfloat16)
    meta = jnp.pad(meta, ((0, 0), (0, META - 3)))
    packed = jnp.concatenate([unit_rows, meta], axis=1)
    send_rows = jnp.zeros((groups, capacity, width + META), jnp.bfloat16)
    send_rows = send_rows.at[owner_group, slot_index - owner_group * capacity].set(packed)
    got_rows = lax.all_to_all(
        send_rows, "dp", split_axis=0, concat_axis=0, tiled=True
    ).reshape(slot_count, -1)
    blocks = pair_blocks(got_rows, pairs)
    got_key = slot_keys(got_rows, width, rows_total)
    column = lax.broadcasted_iota(jnp.int32, got_rows.shape, 1)
    query_rows = jnp.where(column < width, got_rows, jnp.zeros_like(got_rows))
    best_seen = jnp.full((slot_count,), -1.0, jnp.float32)
    for block in blocks:
        found = tile_best(
            query_rows, got_key, block, slot_keys(block, width, rows_total), rows_total
        )
        best_seen = jnp.maximum(best_seen, found)
    answered = lax.all_to_all(
        best_seen.reshape(groups, capacity), "dp", split_axis=0, concat_axis=0, tiled=True
    )
    mine = slot_index[:, None] == jnp.arange(slot_count, dtype=jnp.int32)[None, :]
    return jnp.max(jnp.where(mine, answered.reshape(1, slot_count), -jnp.inf), axis=1)


def solution(mesh):
    in_specs = (P(("dp", "pair"), None), P(("dp", "pair")), P(("dp", "pair")))
    out_specs = P(("dp", "pair"))
    return jax.shard_map(
        on_device, mesh=mesh, in_specs=in_specs, out_specs=out_specs, check_vma=False
    )
```

```python
import jax
import jax.numpy as jnp
from jax import lax
from jax.sharding import PartitionSpec as P

CL_OWN = 2
META = 128


def tile_best(own_rows, own_key, other_rows, other_key, rows_total):
    scores = jnp.dot(own_rows, other_rows.T, preferred_element_type=jnp.float32)
    same_cluster = (other_key[None, :] // rows_total) == (own_key[:, None] // rows_total)
    earlier = same_cluster & (other_key[None, :] < own_key[:, None])
    return jnp.max(jnp.where(earlier, scores, -1.0), axis=1)


def slot_keys(rows, width, rows_total):
    meta = rows[:, width : width + 3].astype(jnp.int32)
    return meta[:, 0] * rows_total + meta[:, 1] * 256 + meta[:, 2]


def pair_blocks(block, pairs):
    chips = pairs // 2
    if pairs % 2 or chips != 4:
        gathered = lax.all_gather(block, "pair", axis=0, tiled=True)
        return jnp.split(gathered, pairs, axis=0)

    def at(y, c):
        return (y % chips) * 2 + c

    def perm(to):
        return [(p, to(p // 2, p % 2)) for p in range(pairs)]

    swap = perm(lambda y, c: at(y, 1 - c))
    up = perm(lambda y, c: at(y + 1, c))
    down = perm(lambda y, c: at(y - 1, c))
    cross = perm(lambda y, c: at(y - 1, 1 - c))
    sibling = lax.ppermute(block, "pair", swap)
    from_below = lax.ppermute(block, "pair", up)
    from_above = lax.ppermute(block, "pair", down)
    two_below = lax.ppermute(from_below, "pair", up)
    two_above = lax.ppermute(from_above, "pair", cross)
    rows = block.shape[0]
    siblings = lax.ppermute(jnp.concatenate([from_below, from_above]), "pair", swap)
    return [block, sibling, from_below, from_above, two_below, two_above, siblings[:rows],
            siblings[rows:]]


def on_device(embedding, labels, order_ids):
    groups = lax.axis_size("dp")
    pairs = lax.axis_size("pair")
    rows_here, width = embedding.shape
    rows_total = rows_here * groups * pairs
    capacity = 2 * rows_here // groups
    slot_count = groups * capacity
    values = embedding.astype(jnp.float32)
    squares = jnp.sum(values * values, axis=1, keepdims=True)
    shifted = squares + 1e-06
    unit_rows = (values * lax.rsqrt(shifted)).astype(jnp.bfloat16)
    owner_group = labels // CL_OWN
    onehot = (owner_group[:, None] == jnp.arange(groups, dtype=jnp.int32)[None, :]).astype(
        jnp.int32
    )
    before = jnp.cumsum(onehot, axis=0) - onehot
    slot_index = owner_group * capacity + jnp.sum(before * onehot, axis=1)
    meta = jnp.stack([labels + 1, order_ids // 256, order_ids % 256], axis=1).astype(jnp.bfloat16)
    meta = jnp.pad(meta, ((0, 0), (0, META - 3)))
    packed = jnp.concatenate([unit_rows, meta], axis=1)
    send_rows = jnp.zeros((slot_count, width + META), jnp.bfloat16).at[slot_index].set(packed)
    got_rows = lax.all_to_all(
        send_rows.reshape(groups, capacity, -1), "dp", split_axis=0, concat_axis=0, tiled=True
    ).reshape(slot_count, -1)
    blocks = pair_blocks(got_rows, pairs)
    got_key = slot_keys(got_rows, width, rows_total)
    column = lax.broadcasted_iota(jnp.int32, got_rows.shape, 1)
    query_rows = jnp.where(column < width, got_rows, jnp.zeros_like(got_rows))
    best_seen = jnp.full((slot_count,), -1.0, jnp.float32)
    for block in blocks:
        found = tile_best(
            query_rows, got_key, block, slot_keys(block, width, rows_total), rows_total
        )
        best_seen = jnp.maximum(best_seen, found)
    answered = lax.all_to_all(
        best_seen.reshape(groups, capacity), "dp", split_axis=0, concat_axis=0, tiled=True
    )
    mine = slot_index[:, None] == jnp.arange(slot_count, dtype=jnp.int32)[None, :]
    return jnp.max(jnp.where(mine, answered.reshape(1, slot_count), -jnp.inf), axis=1)


def solution(mesh):
    in_specs = (P(("dp", "pair"), None), P(("dp", "pair")), P(("dp", "pair")))
    out_specs = P(("dp", "pair"))
    return jax.shard_map(
        on_device, mesh=mesh, in_specs=in_specs, out_specs=out_specs, check_vma=False
    )
```

```python
import jax
import jax.numpy as jnp
from jax import lax
from jax.sharding import PartitionSpec as P

CL_OWN = 2
META = 128


def tile_best(own_rows, own_key, other_rows, other_key, rows_total):
    scores = jnp.dot(own_rows, other_rows.T, preferred_element_type=jnp.float32)
    same_cluster = (other_key[None, :] // rows_total) == (own_key[:, None] // rows_total)
    earlier = same_cluster & (other_key[None, :] < own_key[:, None])
    return jnp.max(jnp.where(earlier, scores, -1.0), axis=1)


def slot_keys(rows, width, rows_total):
    meta = rows[:, width : width + 3].astype(jnp.int32)
    return meta[:, 0] * rows_total + meta[:, 1] * 256 + meta[:, 2]


def pair_blocks(block, pairs):
    chips = pairs // 2
    if pairs % 2 or chips != 4:
        gathered = lax.all_gather(block, "pair", axis=0, tiled=True)
        return jnp.split(gathered, pairs, axis=0)

    def at(y, c):
        return (y % chips) * 2 + c

    def perm(to):
        return [(p, to(p // 2, p % 2)) for p in range(pairs)]

    swap = perm(lambda y, c: at(y, 1 - c))
    up = perm(lambda y, c: at(y + 1, c))
    down = perm(lambda y, c: at(y - 1, c))
    rows = block.shape[0]
    half = rows // 2
    sibling = lax.ppermute(block, "pair", swap)
    from_below = lax.ppermute(block, "pair", up)
    from_above = lax.ppermute(block, "pair", down)
    far_low = lax.ppermute(from_below[:half], "pair", up)
    far_high = lax.ppermute(from_above[half:], "pair", down)
    siblings = lax.ppermute(jnp.concatenate([from_below, from_above]), "pair", swap)
    far = jnp.concatenate([far_low, far_high])
    far_sibling = lax.ppermute(far, "pair", swap)
    return [block, sibling, from_below, from_above, far, far_sibling, siblings[:rows],
            siblings[rows:]]


def on_device(embedding, labels, order_ids):
    groups = lax.axis_size("dp")
    pairs = lax.axis_size("pair")
    rows_here, width = embedding.shape
    rows_total = rows_here * groups * pairs
    capacity = 2 * rows_here // groups
    slot_count = groups * capacity
    values = embedding.astype(jnp.float32)
    squares = jnp.sum(values * values, axis=1, keepdims=True)
    shifted = squares + 1e-06
    unit_rows = (values * lax.rsqrt(shifted)).astype(jnp.bfloat16)
    owner_group = labels // CL_OWN
    onehot = (owner_group[:, None] == jnp.arange(groups, dtype=jnp.int32)[None, :]).astype(
        jnp.int32
    )
    before = jnp.cumsum(onehot, axis=0) - onehot
    slot_index = owner_group * capacity + jnp.sum(before * onehot, axis=1)
    meta = jnp.stack([labels + 1, order_ids // 256, order_ids % 256], axis=1).astype(jnp.bfloat16)
    meta = jnp.pad(meta, ((0, 0), (0, META - 3)))
    packed = jnp.concatenate([unit_rows, meta], axis=1)
    send_rows = jnp.zeros((slot_count, width + META), jnp.bfloat16).at[slot_index].set(packed)
    got_rows = lax.all_to_all(
        send_rows.reshape(groups, capacity, -1), "dp", split_axis=0, concat_axis=0, tiled=True
    ).reshape(slot_count, -1)
    blocks = pair_blocks(got_rows, pairs)
    got_key = slot_keys(got_rows, width, rows_total)
    column = lax.broadcasted_iota(jnp.int32, got_rows.shape, 1)
    query_rows = jnp.where(column < width, got_rows, jnp.zeros_like(got_rows))
    best_seen = jnp.full((slot_count,), -1.0, jnp.float32)
    for block in blocks:
        found = tile_best(
            query_rows, got_key, block, slot_keys(block, width, rows_total), rows_total
        )
        best_seen = jnp.maximum(best_seen, found)
    answered = lax.all_to_all(
        best_seen.reshape(groups, capacity), "dp", split_axis=0, concat_axis=0, tiled=True
    )
    mine = slot_index[:, None] == jnp.arange(slot_count, dtype=jnp.int32)[None, :]
    return jnp.max(jnp.where(mine, answered.reshape(1, slot_count), -jnp.inf), axis=1)


def solution(mesh):
    in_specs = (P(("dp", "pair"), None), P(("dp", "pair")), P(("dp", "pair")))
    out_specs = P(("dp", "pair"))
    return jax.shard_map(
        on_device, mesh=mesh, in_specs=in_specs, out_specs=out_specs, check_vma=False
    )
```

```python
import jax
import jax.numpy as jnp
from jax import lax
from jax.sharding import PartitionSpec as P

CL_OWN = 2
META = 128
LANES = 128


def tile_best(own_rows, own_key, other_rows, other_key, rows_total):
    scores = jnp.dot(own_rows, other_rows.T, preferred_element_type=jnp.float32)
    same_cluster = (other_key[None, :] // rows_total) == (own_key[:, None] // rows_total)
    earlier = same_cluster & (other_key[None, :] < own_key[:, None])
    return jnp.max(jnp.where(earlier, scores, -1.0), axis=1)


def slot_keys(rows, width, rows_total):
    meta = rows[:, width : width + 3].astype(jnp.int32)
    return meta[:, 0] * rows_total + meta[:, 1] * 256 + meta[:, 2]


def pair_blocks(block, pairs):
    chips = pairs // 2
    if pairs % 2 or chips != 4:
        gathered = lax.all_gather(block, "pair", axis=0, tiled=True)
        return jnp.split(gathered, pairs, axis=0)

    def at(y, c):
        return (y % chips) * 2 + c

    def perm(to):
        return [(p, to(p // 2, p % 2)) for p in range(pairs)]

    swap = perm(lambda y, c: at(y, 1 - c))
    up = perm(lambda y, c: at(y + 1, c))
    down = perm(lambda y, c: at(y - 1, c))
    rows = block.shape[0]
    half = rows // 2
    from_below = lax.ppermute(block, "pair", up)
    from_above = lax.ppermute(block, "pair", down)
    far_low = lax.ppermute(from_below[:half], "pair", up)
    far_high = lax.ppermute(from_above[half:], "pair", down)
    siblings = lax.ppermute(jnp.concatenate([block, from_below, from_above]), "pair", swap)
    far = jnp.concatenate([far_low, far_high])
    far_sibling = lax.ppermute(far, "pair", swap)
    return [block, from_below, from_above, far, far_sibling, siblings[:rows],
            siblings[rows : 2 * rows], siblings[2 * rows :]]


def on_device(embedding, labels, order_ids):
    groups = lax.axis_size("dp")
    pairs = lax.axis_size("pair")
    rows_here, width = embedding.shape
    rows_total = rows_here * groups * pairs
    capacity = 2 * rows_here // groups
    slot_count = groups * capacity
    values = embedding.astype(jnp.float32)
    squares = jnp.sum(values * values, axis=1, keepdims=True)
    shifted = squares + 1e-06
    unit_rows = (values * lax.rsqrt(shifted)).astype(jnp.bfloat16)
    owner_group = labels // CL_OWN
    onehot = (owner_group[:, None] == jnp.arange(groups, dtype=jnp.int32)[None, :]).astype(
        jnp.int32
    )
    before = jnp.cumsum(onehot, axis=0) - onehot
    slot_index = owner_group * capacity + jnp.sum(before * onehot, axis=1)
    meta = jnp.stack([labels + 1, order_ids // 256, order_ids % 256], axis=1).astype(jnp.bfloat16)
    meta = jnp.pad(meta, ((0, 0), (0, META - 3)))
    packed = jnp.concatenate([unit_rows, meta], axis=1)
    send_rows = jnp.zeros((slot_count, width + META), jnp.bfloat16).at[slot_index].set(packed)
    got_rows = lax.all_to_all(
        send_rows.reshape(groups, capacity, -1), "dp", split_axis=0, concat_axis=0, tiled=True
    ).reshape(slot_count, -1)
    blocks = pair_blocks(got_rows, pairs)
    got_key = slot_keys(got_rows, width, rows_total)
    column = lax.broadcasted_iota(jnp.int32, got_rows.shape, 1)
    query_rows = jnp.where(column < width, got_rows, jnp.zeros_like(got_rows))
    best_seen = jnp.full((slot_count,), -1.0, jnp.float32)
    for block in blocks:
        found = tile_best(
            query_rows, got_key, block, slot_keys(block, width, rows_total), rows_total
        )
        best_seen = jnp.maximum(best_seen, found)
    lanes = jnp.pad(best_seen.reshape(groups, capacity), ((0, 0), (0, LANES - capacity)))
    answered = lax.all_to_all(lanes, "dp", split_axis=0, concat_axis=0, tiled=True)
    answered = answered[:, :capacity].reshape(1, slot_count)
    mine = slot_index[:, None] == jnp.arange(slot_count, dtype=jnp.int32)[None, :]
    return jnp.max(jnp.where(mine, answered, -jnp.inf), axis=1)


def solution(mesh):
    in_specs = (P(("dp", "pair"), None), P(("dp", "pair")), P(("dp", "pair")))
    out_specs = P(("dp", "pair"))
    return jax.shard_map(
        on_device, mesh=mesh, in_specs=in_specs, out_specs=out_specs, check_vma=False
    )
```

```python
import jax
import jax.numpy as jnp
from jax import lax
from jax.sharding import PartitionSpec as P

CL_OWN = 2
META = 128


def tile_best(own_rows, own_key, other_rows, other_key, rows_total):
    scores = jnp.dot(own_rows, other_rows.T, preferred_element_type=jnp.float32)
    same_cluster = (other_key[None, :] // rows_total) == (own_key[:, None] // rows_total)
    earlier = same_cluster & (other_key[None, :] < own_key[:, None])
    return jnp.max(jnp.where(earlier, scores, -1.0), axis=1)


def slot_keys(rows, width, rows_total):
    meta = rows[:, width : width + 3].astype(jnp.int32)
    return meta[:, 0] * rows_total + meta[:, 1] * 256 + meta[:, 2]


def pair_blocks(block, pairs):
    chips = pairs // 2
    if pairs % 2 or chips != 4:
        gathered = lax.all_gather(block, "pair", axis=0, tiled=True)
        return jnp.split(gathered, pairs, axis=0)

    def at(y, c):
        return (y % chips) * 2 + c

    def perm(to):
        return [(p, to(p // 2, p % 2)) for p in range(pairs)]

    swap = perm(lambda y, c: at(y, 1 - c))
    up = perm(lambda y, c: at(y + 1, c))
    down = perm(lambda y, c: at(y - 1, c))
    rows = block.shape[0]
    half = rows // 2
    from_below = lax.ppermute(block, "pair", up)
    from_above = lax.ppermute(block, "pair", down)
    far_low = lax.ppermute(from_below[:half], "pair", up)
    far_high = lax.ppermute(from_above[half:], "pair", down)
    siblings = lax.ppermute(jnp.concatenate([block, from_below, from_above]), "pair", swap)
    far = jnp.concatenate([far_low, far_high])
    far_sibling = lax.ppermute(far, "pair", swap)
    return [block, from_below, from_above, far, far_sibling, siblings[:rows],
            siblings[rows : 2 * rows], siblings[2 * rows :]]


def on_device(embedding, labels, order_ids):
    groups = lax.axis_size("dp")
    pairs = lax.axis_size("pair")
    rows_here, width = embedding.shape
    rows_total = rows_here * groups * pairs
    capacity = 2 * rows_here // groups
    slot_count = groups * capacity
    values = embedding.astype(jnp.float32)
    squares = jnp.sum(values * values, axis=1, keepdims=True)
    shifted = squares + 1e-06
    unit_rows = (values * lax.rsqrt(shifted)).astype(jnp.bfloat16)
    owner_group = labels // CL_OWN
    onehot = (owner_group[:, None] == jnp.arange(groups, dtype=jnp.int32)[None, :]).astype(
        jnp.int32
    )
    before = jnp.cumsum(onehot, axis=0) - onehot
    slot_index = owner_group * capacity + jnp.sum(before * onehot, axis=1)
    meta = jnp.stack([labels + 1, order_ids // 256, order_ids % 256], axis=1).astype(jnp.bfloat16)
    meta = jnp.pad(meta, ((0, 0), (0, META - 3)))
    packed = jnp.concatenate([unit_rows, meta], axis=1)
    send_rows = jnp.zeros((slot_count, width + META), jnp.bfloat16).at[slot_index].set(packed)
    got_rows = lax.all_to_all(
        send_rows.reshape(groups, capacity, -1), "dp", split_axis=0, concat_axis=0, tiled=True
    ).reshape(slot_count, -1)
    blocks = pair_blocks(got_rows, pairs)
    got_key = slot_keys(got_rows, width, rows_total)
    column = lax.broadcasted_iota(jnp.int32, got_rows.shape, 1)
    query_rows = jnp.where(column < width, got_rows, jnp.zeros_like(got_rows))
    best_seen = jnp.full((slot_count,), -1.0, jnp.float32)
    for block in blocks:
        found = tile_best(
            query_rows, got_key, block, slot_keys(block, width, rows_total), rows_total
        )
        best_seen = jnp.maximum(best_seen, found)
    answered = lax.all_to_all(
        best_seen.reshape(groups, capacity), "dp", split_axis=0, concat_axis=0, tiled=True
    )
    mine = slot_index[:, None] == jnp.arange(slot_count, dtype=jnp.int32)[None, :]
    return jnp.max(jnp.where(mine, answered.reshape(1, slot_count), -jnp.inf), axis=1)


def solution(mesh):
    in_specs = (P(("dp", "pair"), None), P(("dp", "pair")), P(("dp", "pair")))
    out_specs = P(("dp", "pair"))
    return jax.shard_map(
        on_device, mesh=mesh, in_specs=in_specs, out_specs=out_specs, check_vma=False
    )
```

```python
import jax
import jax.numpy as jnp
from jax import lax
from jax.sharding import PartitionSpec as P

CL_OWN = 2
META = 128


def tile_best(own_rows, own_key, other_rows, other_key, rows_total):
    scores = jnp.dot(own_rows, other_rows.T, preferred_element_type=jnp.float32)
    same_cluster = (other_key[None, :] // rows_total) == (own_key[:, None] // rows_total)
    earlier = same_cluster & (other_key[None, :] < own_key[:, None])
    return jnp.max(jnp.where(earlier, scores, -1.0), axis=1)


def slot_keys(rows, width, rows_total):
    meta = rows[:, width : width + 3].astype(jnp.int32)
    return meta[:, 0] * rows_total + meta[:, 1] * 256 + meta[:, 2]


def pair_blocks(block, pairs):
    chips = pairs // 2
    if pairs % 2 or chips != 4:
        gathered = lax.all_gather(block, "pair", axis=0, tiled=True)
        return jnp.split(gathered, pairs, axis=0)

    def at(y, c):
        return (y % chips) * 2 + c

    def perm(to):
        return [(p, to(p // 2, p % 2)) for p in range(pairs)]

    swap = perm(lambda y, c: at(y, 1 - c))
    up = perm(lambda y, c: at(y + 1, c))
    down = perm(lambda y, c: at(y - 1, c))
    relay = perm(lambda y, c: at(y + 1, c) if c == 0 else at(y - 1, c))
    rows = block.shape[0]
    from_below = lax.ppermute(block, "pair", up)
    from_above = lax.ppermute(block, "pair", down)
    core = lax.axis_index("pair") % 2
    far = lax.ppermute(jnp.where(core == 0, from_below, from_above), "pair", relay)
    siblings = lax.ppermute(jnp.concatenate([block, from_below, from_above]), "pair", swap)
    far_sibling = lax.ppermute(far, "pair", swap)
    return [block, from_below, from_above, far, far_sibling, siblings[:rows],
            siblings[rows : 2 * rows], siblings[2 * rows :]]


def on_device(embedding, labels, order_ids):
    groups = lax.axis_size("dp")
    pairs = lax.axis_size("pair")
    rows_here, width = embedding.shape
    rows_total = rows_here * groups * pairs
    capacity = 2 * rows_here // groups
    slot_count = groups * capacity
    values = embedding.astype(jnp.float32)
    squares = jnp.sum(values * values, axis=1, keepdims=True)
    shifted = squares + 1e-06
    unit_rows = (values * lax.rsqrt(shifted)).astype(jnp.bfloat16)
    owner_group = labels // CL_OWN
    onehot = (owner_group[:, None] == jnp.arange(groups, dtype=jnp.int32)[None, :]).astype(
        jnp.int32
    )
    before = jnp.cumsum(onehot, axis=0) - onehot
    slot_index = owner_group * capacity + jnp.sum(before * onehot, axis=1)
    meta = jnp.stack([labels + 1, order_ids // 256, order_ids % 256], axis=1).astype(jnp.bfloat16)
    meta = jnp.pad(meta, ((0, 0), (0, META - 3)))
    packed = jnp.concatenate([unit_rows, meta], axis=1)
    send_rows = jnp.zeros((slot_count, width + META), jnp.bfloat16).at[slot_index].set(packed)
    got_rows = lax.all_to_all(
        send_rows.reshape(groups, capacity, -1), "dp", split_axis=0, concat_axis=0, tiled=True
    ).reshape(slot_count, -1)
    blocks = pair_blocks(got_rows, pairs)
    got_key = slot_keys(got_rows, width, rows_total)
    column = lax.broadcasted_iota(jnp.int32, got_rows.shape, 1)
    query_rows = jnp.where(column < width, got_rows, jnp.zeros_like(got_rows))
    best_seen = jnp.full((slot_count,), -1.0, jnp.float32)
    for block in blocks:
        found = tile_best(
            query_rows, got_key, block, slot_keys(block, width, rows_total), rows_total
        )
        best_seen = jnp.maximum(best_seen, found)
    answered = lax.all_to_all(
        best_seen.reshape(groups, capacity), "dp", split_axis=0, concat_axis=0, tiled=True
    )
    mine = slot_index[:, None] == jnp.arange(slot_count, dtype=jnp.int32)[None, :]
    return jnp.max(jnp.where(mine, answered.reshape(1, slot_count), -jnp.inf), axis=1)


def solution(mesh):
    in_specs = (P(("dp", "pair"), None), P(("dp", "pair")), P(("dp", "pair")))
    out_specs = P(("dp", "pair"))
    return jax.shard_map(
        on_device, mesh=mesh, in_specs=in_specs, out_specs=out_specs, check_vma=False
    )
```

```python
import jax
import jax.numpy as jnp
from jax import lax
from jax.sharding import PartitionSpec as P

CL_OWN = 2
META = 128
LANES = 128


def tile_best(own_rows, own_key, other_rows, other_key, rows_total):
    scores = jnp.dot(own_rows, other_rows.T, preferred_element_type=jnp.float32)
    same_cluster = (other_key[None, :] // rows_total) == (own_key[:, None] // rows_total)
    earlier = same_cluster & (other_key[None, :] < own_key[:, None])
    return jnp.max(jnp.where(earlier, scores, -1.0), axis=1)


def slot_keys(rows, width, rows_total):
    meta = rows[:, width : width + 3].astype(jnp.int32)
    return meta[:, 0] * rows_total + meta[:, 1] * 256 + meta[:, 2]


def pair_blocks(block, pairs):
    chips = pairs // 2
    if pairs % 2 or chips != 4:
        gathered = lax.all_gather(block, "pair", axis=0, tiled=True)
        return jnp.split(gathered, pairs, axis=0)

    def at(y, c):
        return (y % chips) * 2 + c

    def perm(to):
        return [(p, to(p // 2, p % 2)) for p in range(pairs)]

    swap = perm(lambda y, c: at(y, 1 - c))
    up = perm(lambda y, c: at(y + 1, c))
    down = perm(lambda y, c: at(y - 1, c))
    rows = block.shape[0]
    half = rows // 2
    from_below = lax.ppermute(block, "pair", up)
    from_above = lax.ppermute(block, "pair", down)
    far_low = lax.ppermute(from_below[:half], "pair", up)
    far_high = lax.ppermute(from_above[half:], "pair", down)
    siblings = lax.ppermute(jnp.concatenate([block, from_below, from_above]), "pair", swap)
    far = jnp.concatenate([far_low, far_high])
    far_sibling = lax.ppermute(far, "pair", swap)
    return [block, from_below, from_above, far, far_sibling, siblings]


def on_device(embedding, labels, order_ids):
    groups = lax.axis_size("dp")
    pairs = lax.axis_size("pair")
    rows_here, width = embedding.shape
    rows_total = rows_here * groups * pairs
    capacity = 2 * rows_here // groups
    slot_count = groups * capacity
    values = embedding.astype(jnp.float32)
    squares = jnp.sum(values * values, axis=1, keepdims=True)
    shifted = squares + 1e-06
    unit_rows = (values * lax.rsqrt(shifted)).astype(jnp.bfloat16)
    owner_group = labels // CL_OWN
    onehot = (owner_group[:, None] == jnp.arange(groups, dtype=jnp.int32)[None, :]).astype(
        jnp.int32
    )
    before = jnp.cumsum(onehot, axis=0) - onehot
    slot_index = owner_group * capacity + jnp.sum(before * onehot, axis=1)
    meta_column = lax.broadcasted_iota(jnp.int32, (rows_here, META), 1)
    meta = jnp.where(meta_column == 0, labels[:, None] + 1, 0)
    meta = jnp.where(meta_column == 1, order_ids[:, None] // 256, meta)
    meta = jnp.where(meta_column == 2, order_ids[:, None] % 256, meta).astype(jnp.bfloat16)
    packed = jnp.concatenate([unit_rows, meta], axis=1)
    send_rows = jnp.zeros((slot_count, width + META), jnp.bfloat16).at[slot_index].set(packed)
    got_rows = lax.all_to_all(
        send_rows.reshape(groups, capacity, -1), "dp", split_axis=0, concat_axis=0, tiled=True
    ).reshape(slot_count, -1)
    blocks = pair_blocks(got_rows, pairs)
    got_key = slot_keys(got_rows, width, rows_total)
    column = lax.broadcasted_iota(jnp.int32, got_rows.shape, 1)
    query_rows = jnp.where(column < width, got_rows, jnp.zeros_like(got_rows))
    best_seen = jnp.full((slot_count,), -1.0, jnp.float32)
    for block in blocks:
        found = tile_best(
            query_rows, got_key, block, slot_keys(block, width, rows_total), rows_total
        )
        best_seen = jnp.maximum(best_seen, found)
    lanes = jnp.pad(best_seen.reshape(groups, capacity), ((0, 0), (0, LANES - capacity)))
    answered = lax.all_to_all(lanes, "dp", split_axis=0, concat_axis=0, tiled=True)
    answered = answered[:, :capacity].reshape(1, slot_count)
    mine = slot_index[:, None] == jnp.arange(slot_count, dtype=jnp.int32)[None, :]
    return jnp.max(jnp.where(mine, answered, -jnp.inf), axis=1)


def solution(mesh):
    in_specs = (P(("dp", "pair"), None), P(("dp", "pair")), P(("dp", "pair")))
    out_specs = P(("dp", "pair"))
    return jax.shard_map(
        on_device, mesh=mesh, in_specs=in_specs, out_specs=out_specs, check_vma=False
    )
```

```python
import functools

import jax
import jax.numpy as jnp
from jax import lax
from jax.sharding import PartitionSpec as P

CL_OWN = 2
META = 128
LANES = 128


def tile_best(own_rows, own_key, other_rows, other_key, rows_total):
    scores = jnp.dot(own_rows, other_rows.T, preferred_element_type=jnp.float32)
    same_cluster = (other_key[None, :] // rows_total) == (own_key[:, None] // rows_total)
    earlier = same_cluster & (other_key[None, :] < own_key[:, None])
    return jnp.max(jnp.where(earlier, scores, -1.0), axis=1)


def slot_keys(rows, width, rows_total):
    meta = rows[:, width : width + 3].astype(jnp.int32)
    return meta[:, 0] * rows_total + meta[:, 1] * 256 + meta[:, 2]


def query_view(rows, width):
    column = lax.broadcasted_iota(jnp.int32, rows.shape, 1)
    return jnp.where(column < width, rows, jnp.zeros_like(rows))


def pair_best(block, width, rows_total, pairs):
    own_key = slot_keys(block, width, rows_total)
    own_query = query_view(block, width)
    chips = pairs // 2
    if pairs % 2 or chips != 4:
        gathered = lax.all_gather(block, "pair", axis=0, tiled=True)
        return tile_best(own_query, own_key, gathered, slot_keys(gathered, width, rows_total),
                         rows_total)

    def at(y, c):
        return (y % chips) * 2 + c

    def perm(to):
        return [(p, to(p // 2, p % 2)) for p in range(pairs)]

    swap = perm(lambda y, c: at(y, 1 - c))
    up = perm(lambda y, c: at(y + 1, c))
    down = perm(lambda y, c: at(y - 1, c))
    rows = block.shape[0]
    from_below = lax.ppermute(block, "pair", up)
    from_above = lax.ppermute(block, "pair", down)
    swapped = lax.ppermute(jnp.concatenate([block, from_above]), "pair", swap)
    sibling, sibling_above = swapped[:rows], swapped[rows:]

    def best_over(query, query_key, keys):
        found = [tile_best(query, query_key, k, slot_keys(k, width, rows_total), rows_total)
                 for k in keys]
        return functools.reduce(jnp.maximum, found)

    best = best_over(own_query, own_key, [block, from_below, from_above, sibling])
    for_sibling = best_over(query_view(sibling, width), slot_keys(sibling, width, rows_total),
                            [from_below, from_above])
    for_below = best_over(query_view(from_below, width),
                          slot_keys(from_below, width, rows_total),
                          [from_above, sibling_above])
    from_sibling = lax.ppermute(for_sibling, "pair", swap)
    from_chip_above = lax.ppermute(for_below, "pair", down)
    return jnp.maximum(best, jnp.maximum(from_sibling, from_chip_above))


def on_device(embedding, labels, order_ids):
    groups = lax.axis_size("dp")
    pairs = lax.axis_size("pair")
    rows_here, width = embedding.shape
    rows_total = rows_here * groups * pairs
    capacity = 2 * rows_here // groups
    slot_count = groups * capacity
    values = embedding.astype(jnp.float32)
    squares = jnp.sum(values * values, axis=1, keepdims=True)
    shifted = squares + 1e-06
    unit_rows = (values * lax.rsqrt(shifted)).astype(jnp.bfloat16)
    owner_group = labels // CL_OWN
    onehot = (owner_group[:, None] == jnp.arange(groups, dtype=jnp.int32)[None, :]).astype(
        jnp.int32
    )
    before = jnp.cumsum(onehot, axis=0) - onehot
    slot_index = owner_group * capacity + jnp.sum(before * onehot, axis=1)
    meta_column = lax.broadcasted_iota(jnp.int32, (rows_here, META), 1)
    meta = jnp.where(meta_column == 0, labels[:, None] + 1, 0)
    meta = jnp.where(meta_column == 1, order_ids[:, None] // 256, meta)
    meta = jnp.where(meta_column == 2, order_ids[:, None] % 256, meta).astype(jnp.bfloat16)
    packed = jnp.concatenate([unit_rows, meta], axis=1)
    send_rows = jnp.zeros((slot_count, width + META), jnp.bfloat16).at[slot_index].set(packed)
    got_rows = lax.all_to_all(
        send_rows.reshape(groups, capacity, -1), "dp", split_axis=0, concat_axis=0, tiled=True
    ).reshape(slot_count, -1)
    best_seen = pair_best(got_rows, width, rows_total, pairs)
    lanes = jnp.pad(best_seen.reshape(groups, capacity), ((0, 0), (0, LANES - capacity)))
    answered = lax.all_to_all(lanes, "dp", split_axis=0, concat_axis=0, tiled=True)
    answered = answered[:, :capacity].reshape(1, slot_count)
    mine = slot_index[:, None] == jnp.arange(slot_count, dtype=jnp.int32)[None, :]
    return jnp.max(jnp.where(mine, answered, -jnp.inf), axis=1)


def solution(mesh):
    in_specs = (P(("dp", "pair"), None), P(("dp", "pair")), P(("dp", "pair")))
    out_specs = P(("dp", "pair"))
    return jax.shard_map(
        on_device, mesh=mesh, in_specs=in_specs, out_specs=out_specs, check_vma=False
    )
```

```python
import functools

import jax
import jax.numpy as jnp
from jax import lax
from jax.sharding import PartitionSpec as P

CL_OWN = 2
META = 128
LANES = 128
META_ROWS = 16


def tile_best(own_rows, own_key, other_rows, other_key, rows_total):
    scores = jnp.dot(own_rows, other_rows.T, preferred_element_type=jnp.float32)
    same_cluster = (other_key[None, :] // rows_total) == (own_key[:, None] // rows_total)
    earlier = same_cluster & (other_key[None, :] < own_key[:, None])
    return jnp.max(jnp.where(earlier, scores, -1.0), axis=1)


def to_block(got, width):
    slots = got.shape[0]
    meta = got[:, width : width + 3].T
    meta = jnp.pad(meta, ((0, META_ROWS - 3), (0, width - slots)))
    return jnp.concatenate([got[:, :width], meta], axis=0)


def block_best(query_block, key_block, slots, rows_total):
    query_key = block_keys(query_block, slots, rows_total)
    key_key = block_keys(key_block, slots, rows_total)
    return tile_best(query_block[:slots], query_key, key_block[:slots], key_key, rows_total)


def block_keys(block, slots, rows_total):
    meta = block[slots : slots + 3, :slots].astype(jnp.int32)
    return meta[0] * rows_total + meta[1] * 256 + meta[2]


def pair_best(block, slots, rows_total, pairs):
    chips = pairs // 2
    if pairs % 2 or chips != 4:
        gathered = lax.all_gather(block, "pair", axis=0, tiled=False)
        found = [block_best(block, gathered[i], slots, rows_total) for i in range(pairs)]
        return functools.reduce(jnp.maximum, found)

    def at(y, c):
        return (y % chips) * 2 + c

    def perm(to):
        return [(p, to(p // 2, p % 2)) for p in range(pairs)]

    swap = perm(lambda y, c: at(y, 1 - c))
    up = perm(lambda y, c: at(y + 1, c))
    down = perm(lambda y, c: at(y - 1, c))
    rows = block.shape[0]
    from_below = lax.ppermute(block, "pair", up)
    from_above = lax.ppermute(block, "pair", down)
    swapped = lax.ppermute(jnp.concatenate([block, from_above]), "pair", swap)
    sibling, sibling_above = swapped[:rows], swapped[rows:]

    def best_over(query, keys):
        found = [block_best(query, k, slots, rows_total) for k in keys]
        return functools.reduce(jnp.maximum, found)

    best = best_over(block, [block, from_below, from_above, sibling])
    for_sibling = best_over(sibling, [from_below, from_above])
    for_below = best_over(from_below, [from_above, sibling_above])
    from_sibling = lax.ppermute(for_sibling, "pair", swap)
    from_chip_above = lax.ppermute(for_below, "pair", down)
    return jnp.maximum(best, jnp.maximum(from_sibling, from_chip_above))


def on_device(embedding, labels, order_ids):
    groups = lax.axis_size("dp")
    pairs = lax.axis_size("pair")
    rows_here, width = embedding.shape
    rows_total = rows_here * groups * pairs
    capacity = 2 * rows_here // groups
    slot_count = groups * capacity
    values = embedding.astype(jnp.float32)
    squares = jnp.sum(values * values, axis=1, keepdims=True)
    shifted = squares + 1e-06
    unit_rows = (values * lax.rsqrt(shifted)).astype(jnp.bfloat16)
    owner_group = labels // CL_OWN
    onehot = (owner_group[:, None] == jnp.arange(groups, dtype=jnp.int32)[None, :]).astype(
        jnp.int32
    )
    before = jnp.cumsum(onehot, axis=0) - onehot
    slot_index = owner_group * capacity + jnp.sum(before * onehot, axis=1)
    meta_column = lax.broadcasted_iota(jnp.int32, (rows_here, META), 1)
    meta = jnp.where(meta_column == 0, labels[:, None] + 1, 0)
    meta = jnp.where(meta_column == 1, order_ids[:, None] // 256, meta)
    meta = jnp.where(meta_column == 2, order_ids[:, None] % 256, meta).astype(jnp.bfloat16)
    packed = jnp.concatenate([unit_rows, meta], axis=1)
    send_rows = jnp.zeros((slot_count, width + META), jnp.bfloat16).at[slot_index].set(packed)
    got_rows = lax.all_to_all(
        send_rows.reshape(groups, capacity, -1), "dp", split_axis=0, concat_axis=0, tiled=True
    ).reshape(slot_count, -1)
    best_seen = pair_best(to_block(got_rows, width), slot_count, rows_total, pairs)
    lanes = jnp.pad(best_seen.reshape(groups, capacity), ((0, 0), (0, LANES - capacity)))
    answered = lax.all_to_all(lanes, "dp", split_axis=0, concat_axis=0, tiled=True)
    answered = answered[:, :capacity].reshape(1, slot_count)
    mine = slot_index[:, None] == jnp.arange(slot_count, dtype=jnp.int32)[None, :]
    return jnp.max(jnp.where(mine, answered, -jnp.inf), axis=1)


def solution(mesh):
    in_specs = (P(("dp", "pair"), None), P(("dp", "pair")), P(("dp", "pair")))
    out_specs = P(("dp", "pair"))
    return jax.shard_map(
        on_device, mesh=mesh, in_specs=in_specs, out_specs=out_specs, check_vma=False
    )
```

```python
import functools

import jax
import jax.numpy as jnp
from jax import lax
from jax.sharding import PartitionSpec as P

CL_OWN = 2
META = 128
LANES = 128
META_ROWS = 16


def tile_best(own_rows, own_key, other_rows, other_key, rows_total):
    scores = jnp.dot(own_rows, other_rows.T, preferred_element_type=jnp.float32)
    same_cluster = (other_key[None, :] // rows_total) == (own_key[:, None] // rows_total)
    earlier = same_cluster & (other_key[None, :] < own_key[:, None])
    return jnp.max(jnp.where(earlier, scores, -1.0), axis=1)


def to_block(got, width):
    slots = got.shape[0]
    meta = got[:, width : width + 3].T
    meta = jnp.pad(meta, ((0, META_ROWS - 3), (0, width - slots)))
    return jnp.concatenate([got[:, :width], meta], axis=0)


def block_best(query_block, key_block, slots, rows_total):
    query_key = block_keys(query_block, slots, rows_total)
    key_key = block_keys(key_block, slots, rows_total)
    return tile_best(query_block[:slots], query_key, key_block[:slots], key_key, rows_total)


def block_keys(block, slots, rows_total):
    meta = block[slots : slots + 3, :slots].astype(jnp.int32)
    return meta[0] * rows_total + meta[1] * 256 + meta[2]


def pair_best(block, slots, rows_total, pairs):
    chips = pairs // 2
    if pairs % 2 or chips != 4:
        gathered = lax.all_gather(block, "pair", axis=0, tiled=False)
        found = [block_best(block, gathered[i], slots, rows_total) for i in range(pairs)]
        return functools.reduce(jnp.maximum, found)

    def at(y, c):
        return (y % chips) * 2 + c

    def perm(to):
        return [(p, to(p // 2, p % 2)) for p in range(pairs)]

    swap = perm(lambda y, c: at(y, 1 - c))
    up = perm(lambda y, c: at(y + 1, c))
    down = perm(lambda y, c: at(y - 1, c))
    rows = block.shape[0]
    from_below = lax.ppermute(block, "pair", up)
    from_above = lax.ppermute(block, "pair", down)
    swapped = lax.ppermute(jnp.concatenate([block, from_above, from_below]), "pair", swap)
    sibling, sibling_above = swapped[:rows], swapped[rows : 2 * rows]
    sibling_below = swapped[2 * rows :]

    def best_over(query, keys):
        found = [block_best(query, k, slots, rows_total) for k in keys]
        return functools.reduce(jnp.maximum, found)

    best = best_over(
        block, [block, from_below, from_above, sibling, sibling_above, sibling_below]
    )
    for_below = best_over(from_below, [from_above, sibling_above])
    from_chip_above = lax.ppermute(for_below, "pair", down)
    return jnp.maximum(best, from_chip_above)


def on_device(embedding, labels, order_ids):
    groups = lax.axis_size("dp")
    pairs = lax.axis_size("pair")
    rows_here, width = embedding.shape
    rows_total = rows_here * groups * pairs
    capacity = 2 * rows_here // groups
    slot_count = groups * capacity
    values = embedding.astype(jnp.float32)
    squares = jnp.sum(values * values, axis=1, keepdims=True)
    shifted = squares + 1e-06
    unit_rows = (values * lax.rsqrt(shifted)).astype(jnp.bfloat16)
    owner_group = labels // CL_OWN
    onehot = (owner_group[:, None] == jnp.arange(groups, dtype=jnp.int32)[None, :]).astype(
        jnp.int32
    )
    before = jnp.cumsum(onehot, axis=0) - onehot
    slot_index = owner_group * capacity + jnp.sum(before * onehot, axis=1)
    meta_column = lax.broadcasted_iota(jnp.int32, (rows_here, META), 1)
    meta = jnp.where(meta_column == 0, labels[:, None] + 1, 0)
    meta = jnp.where(meta_column == 1, order_ids[:, None] // 256, meta)
    meta = jnp.where(meta_column == 2, order_ids[:, None] % 256, meta).astype(jnp.bfloat16)
    packed = jnp.concatenate([unit_rows, meta], axis=1)
    send_rows = jnp.zeros((slot_count, width + META), jnp.bfloat16).at[slot_index].set(packed)
    got_rows = lax.all_to_all(
        send_rows.reshape(groups, capacity, -1), "dp", split_axis=0, concat_axis=0, tiled=True
    ).reshape(slot_count, -1)
    best_seen = pair_best(to_block(got_rows, width), slot_count, rows_total, pairs)
    lanes = jnp.pad(best_seen.reshape(groups, capacity), ((0, 0), (0, LANES - capacity)))
    answered = lax.all_to_all(lanes, "dp", split_axis=0, concat_axis=0, tiled=True)
    answered = answered[:, :capacity].reshape(1, slot_count)
    mine = slot_index[:, None] == jnp.arange(slot_count, dtype=jnp.int32)[None, :]
    return jnp.max(jnp.where(mine, answered, -jnp.inf), axis=1)


def solution(mesh):
    in_specs = (P(("dp", "pair"), None), P(("dp", "pair")), P(("dp", "pair")))
    out_specs = P(("dp", "pair"))
    return jax.shard_map(
        on_device, mesh=mesh, in_specs=in_specs, out_specs=out_specs, check_vma=False
    )
```

```python
import functools

import jax
import jax.numpy as jnp
from jax import lax
from jax.sharding import PartitionSpec as P

CL_OWN = 2
META = 128
LANES = 128
META_ROWS = 16


def tile_best(own_rows, own_key, other_rows, other_key, rows_total):
    scores = jnp.dot(own_rows, other_rows.T, preferred_element_type=jnp.float32)
    same_cluster = (other_key[None, :] // rows_total) == (own_key[:, None] // rows_total)
    earlier = same_cluster & (other_key[None, :] < own_key[:, None])
    return jnp.max(jnp.where(earlier, scores, -1.0), axis=1)


def to_block(got, width):
    slots = got.shape[0]
    meta = got[:, width : width + 3].T
    meta = jnp.pad(meta, ((0, META_ROWS - 3), (0, width - slots)))
    return jnp.concatenate([got[:, :width], meta], axis=0)


def block_best(query_block, key_block, slots, rows_total):
    query_key = block_keys(query_block, slots, rows_total)
    key_key = block_keys(key_block, slots, rows_total)
    return tile_best(query_block[:slots], query_key, key_block[:slots], key_key, rows_total)


def block_keys(block, slots, rows_total):
    meta = block[slots : slots + 3, :slots].astype(jnp.int32)
    return meta[0] * rows_total + meta[1] * 256 + meta[2]


def pair_best(block, slots, rows_total, pairs):
    chips = pairs // 2
    if pairs % 2 or chips != 4:
        gathered = lax.all_gather(block, "pair", axis=0, tiled=False)
        found = [block_best(block, gathered[i], slots, rows_total) for i in range(pairs)]
        return functools.reduce(jnp.maximum, found)

    def at(y, c):
        return (y % chips) * 2 + c

    def perm(to):
        return [(p, to(p // 2, p % 2)) for p in range(pairs)]

    swap = perm(lambda y, c: at(y, 1 - c))
    up = perm(lambda y, c: at(y + 1, c))
    down = perm(lambda y, c: at(y - 1, c))
    rows = block.shape[0]
    from_below = lax.ppermute(block, "pair", up)
    from_above = lax.ppermute(block, "pair", down)
    swapped = lax.ppermute(jnp.concatenate([block, from_above, from_below]), "pair", swap)
    sibling, sibling_above = swapped[:rows], swapped[rows : 2 * rows]
    sibling_below = swapped[2 * rows :]

    def best_over(query, keys):
        found = [block_best(query, k, slots, rows_total) for k in keys]
        return functools.reduce(jnp.maximum, found)

    best = best_over(
        block, [block, from_below, from_above, sibling, sibling_above, sibling_below]
    )
    for_below = best_over(from_below, [from_above, sibling_above])
    from_chip_above = lax.ppermute(for_below, "pair", down)
    return jnp.maximum(best, from_chip_above)


def on_device(embedding, labels, order_ids):
    groups = lax.axis_size("dp")
    pairs = lax.axis_size("pair")
    rows_here, width = embedding.shape
    rows_total = rows_here * groups * pairs
    capacity = 2 * rows_here // groups
    slot_count = groups * capacity
    values = embedding.astype(jnp.float32)
    gram = jnp.dot(embedding, embedding.T, preferred_element_type=jnp.float32)
    diagonal = lax.broadcasted_iota(jnp.int32, gram.shape, 0) == lax.broadcasted_iota(
        jnp.int32, gram.shape, 1
    )
    squares = jnp.sum(jnp.where(diagonal, gram, 0.0), axis=1, keepdims=True)
    shifted = squares + 1e-06
    unit_rows = (values * lax.rsqrt(shifted)).astype(jnp.bfloat16)
    owner_group = labels // CL_OWN
    onehot = (owner_group[:, None] == jnp.arange(groups, dtype=jnp.int32)[None, :]).astype(
        jnp.int32
    )
    before = jnp.cumsum(onehot, axis=0) - onehot
    slot_index = owner_group * capacity + jnp.sum(before * onehot, axis=1)
    meta_column = lax.broadcasted_iota(jnp.int32, (rows_here, META), 1)
    meta = jnp.where(meta_column == 0, labels[:, None] + 1, 0)
    meta = jnp.where(meta_column == 1, order_ids[:, None] // 256, meta)
    meta = jnp.where(meta_column == 2, order_ids[:, None] % 256, meta).astype(jnp.bfloat16)
    packed = jnp.concatenate([unit_rows, meta], axis=1)
    send_rows = jnp.zeros((slot_count, width + META), jnp.bfloat16).at[slot_index].set(packed)
    got_rows = lax.all_to_all(
        send_rows.reshape(groups, capacity, -1), "dp", split_axis=0, concat_axis=0, tiled=True
    ).reshape(slot_count, -1)
    best_seen = pair_best(to_block(got_rows, width), slot_count, rows_total, pairs)
    lanes = jnp.pad(best_seen.reshape(groups, capacity), ((0, 0), (0, LANES - capacity)))
    answered = lax.all_to_all(lanes, "dp", split_axis=0, concat_axis=0, tiled=True)
    answered = answered[:, :capacity].reshape(1, slot_count)
    mine = slot_index[:, None] == jnp.arange(slot_count, dtype=jnp.int32)[None, :]
    return jnp.max(jnp.where(mine, answered, -jnp.inf), axis=1)


def solution(mesh):
    in_specs = (P(("dp", "pair"), None), P(("dp", "pair")), P(("dp", "pair")))
    out_specs = P(("dp", "pair"))
    return jax.shard_map(
        on_device, mesh=mesh, in_specs=in_specs, out_specs=out_specs, check_vma=False
    )
```

```python
import functools

import jax
import jax.numpy as jnp
from jax import lax
from jax.sharding import PartitionSpec as P

CL_OWN = 2
META = 128
LANES = 128
META_ROWS = 16


def tile_best(own_rows, own_key, other_rows, other_key, rows_total):
    scores = jnp.dot(own_rows, other_rows.T, preferred_element_type=jnp.float32)
    same_cluster = (other_key[None, :] // rows_total) == (own_key[:, None] // rows_total)
    earlier = same_cluster & (other_key[None, :] < own_key[:, None])
    return jnp.max(jnp.where(earlier, scores, -1.0), axis=1)


def to_block(got, width):
    slots = got.shape[0]
    meta = got[:, width : width + 3].T
    meta = jnp.pad(meta, ((0, META_ROWS - 3), (0, width - slots)))
    return jnp.concatenate([got[:, :width], meta], axis=0)


def block_best(query_block, key_block, slots, rows_total):
    query_key = block_keys(query_block, slots, rows_total)
    key_key = block_keys(key_block, slots, rows_total)
    return tile_best(query_block[:slots], query_key, key_block[:slots], key_key, rows_total)


def block_keys(block, slots, rows_total):
    meta = block[slots : slots + 3, :slots].astype(jnp.int32)
    return meta[0] * rows_total + meta[1] * 256 + meta[2]


def pair_best(block, slots, rows_total, pairs):
    chips = pairs // 2
    if pairs % 2 or chips != 4:
        gathered = lax.all_gather(block, "pair", axis=0, tiled=False)
        found = [block_best(block, gathered[i], slots, rows_total) for i in range(pairs)]
        return functools.reduce(jnp.maximum, found)

    def at(y, c):
        return (y % chips) * 2 + c

    def perm(to):
        return [(p, to(p // 2, p % 2)) for p in range(pairs)]

    swap = perm(lambda y, c: at(y, 1 - c))
    up = perm(lambda y, c: at(y + 1, c))
    down = perm(lambda y, c: at(y - 1, c))
    rows = block.shape[0]
    from_below = lax.ppermute(block, "pair", up)
    from_above = lax.ppermute(block, "pair", down)
    swapped = lax.ppermute(jnp.concatenate([block, from_above]), "pair", swap)
    sibling, sibling_above = swapped[:rows], swapped[rows:]

    def best_over(query, keys):
        found = [block_best(query, k, slots, rows_total) for k in keys]
        return functools.reduce(jnp.maximum, found)

    for_below = best_over(from_below, [from_above, sibling_above])
    from_chip_above = lax.ppermute(for_below, "pair", down)
    sibling, _ = lax.optimization_barrier((sibling, for_below))
    best = best_over(block, [block, from_below, from_above, sibling])
    for_sibling = best_over(sibling, [from_below, from_above])
    from_sibling = lax.ppermute(for_sibling, "pair", swap)
    return jnp.maximum(best, jnp.maximum(from_sibling, from_chip_above))


def on_device(embedding, labels, order_ids):
    groups = lax.axis_size("dp")
    pairs = lax.axis_size("pair")
    rows_here, width = embedding.shape
    rows_total = rows_here * groups * pairs
    capacity = 2 * rows_here // groups
    slot_count = groups * capacity
    values = embedding.astype(jnp.float32)
    squares = jnp.sum(values * values, axis=1, keepdims=True)
    shifted = squares + 1e-06
    unit_rows = (values * lax.rsqrt(shifted)).astype(jnp.bfloat16)
    owner_group = labels // CL_OWN
    onehot = (owner_group[:, None] == jnp.arange(groups, dtype=jnp.int32)[None, :]).astype(
        jnp.int32
    )
    before = jnp.cumsum(onehot, axis=0) - onehot
    slot_index = owner_group * capacity + jnp.sum(before * onehot, axis=1)
    meta_column = lax.broadcasted_iota(jnp.int32, (rows_here, META), 1)
    meta = jnp.where(meta_column == 0, labels[:, None] + 1, 0)
    meta = jnp.where(meta_column == 1, order_ids[:, None] // 256, meta)
    meta = jnp.where(meta_column == 2, order_ids[:, None] % 256, meta).astype(jnp.bfloat16)
    packed = jnp.concatenate([unit_rows, meta], axis=1)
    send_rows = jnp.zeros((slot_count, width + META), jnp.bfloat16).at[slot_index].set(packed)
    got_rows = lax.all_to_all(
        send_rows.reshape(groups, capacity, -1), "dp", split_axis=0, concat_axis=0, tiled=True
    ).reshape(slot_count, -1)
    best_seen = pair_best(to_block(got_rows, width), slot_count, rows_total, pairs)
    lanes = jnp.pad(best_seen.reshape(groups, capacity), ((0, 0), (0, LANES - capacity)))
    answered = lax.all_to_all(lanes, "dp", split_axis=0, concat_axis=0, tiled=True)
    answered = answered[:, :capacity].reshape(1, slot_count)
    mine = slot_index[:, None] == jnp.arange(slot_count, dtype=jnp.int32)[None, :]
    return jnp.max(jnp.where(mine, answered, -jnp.inf), axis=1)


def solution(mesh):
    in_specs = (P(("dp", "pair"), None), P(("dp", "pair")), P(("dp", "pair")))
    out_specs = P(("dp", "pair"))
    return jax.shard_map(
        on_device, mesh=mesh, in_specs=in_specs, out_specs=out_specs, check_vma=False
    )
```

```python
import functools

import jax
import jax.numpy as jnp
from jax import lax
from jax.sharding import PartitionSpec as P

CL_OWN = 2
META = 128
LANES = 128
META_ROWS = 16


def tile_best(own_rows, own_key, other_rows, other_key, rows_total):
    scores = jnp.dot(own_rows, other_rows.T, preferred_element_type=jnp.float32)
    same_cluster = (other_key[None, :] // rows_total) == (own_key[:, None] // rows_total)
    earlier = same_cluster & (other_key[None, :] < own_key[:, None])
    return jnp.max(jnp.where(earlier, scores, -1.0), axis=1)


def to_block(got, width):
    slots = got.shape[0]
    meta = got[:, width : width + 3].T
    meta = jnp.pad(meta, ((0, META_ROWS - 3), (0, width - slots)))
    return jnp.concatenate([got[:, :width], meta], axis=0)


def block_best(query_block, key_block, slots, rows_total):
    query_key = block_keys(query_block, slots, rows_total)
    key_key = block_keys(key_block, slots, rows_total)
    return tile_best(query_block[:slots], query_key, key_block[:slots], key_key, rows_total)


def block_keys(block, slots, rows_total):
    meta = block[slots : slots + 3, :slots].astype(jnp.int32)
    return meta[0] * rows_total + meta[1] * 256 + meta[2]


def pair_best(block, slots, rows_total, pairs):
    chips = pairs // 2
    if pairs % 2 or chips != 4:
        gathered = lax.all_gather(block, "pair", axis=0, tiled=False)
        found = [block_best(block, gathered[i], slots, rows_total) for i in range(pairs)]
        return functools.reduce(jnp.maximum, found)

    def at(y, c):
        return (y % chips) * 2 + c

    def perm(to):
        return [(p, to(p // 2, p % 2)) for p in range(pairs)]

    swap = perm(lambda y, c: at(y, 1 - c))
    up = perm(lambda y, c: at(y + 1, c))
    down = perm(lambda y, c: at(y - 1, c))
    rows = block.shape[0]
    from_below = lax.ppermute(block, "pair", up)
    from_above = lax.ppermute(block, "pair", down)
    swapped = lax.ppermute(jnp.concatenate([block, from_above]), "pair", swap)
    sibling, sibling_above = swapped[:rows], swapped[rows:]

    def best_over(query, keys):
        found = [block_best(query, k, slots, rows_total) for k in keys]
        return functools.reduce(jnp.maximum, found)

    sibling_below = lax.ppermute(from_below, "pair", swap)
    for_below = best_over(from_below, [from_above, sibling_above])
    from_chip_above = lax.ppermute(for_below, "pair", down)
    sibling, sibling_below, _ = lax.optimization_barrier((sibling, sibling_below, for_below))
    best = best_over(
        block, [block, from_below, from_above, sibling, sibling_above, sibling_below]
    )
    return jnp.maximum(best, from_chip_above)


def on_device(embedding, labels, order_ids):
    groups = lax.axis_size("dp")
    pairs = lax.axis_size("pair")
    rows_here, width = embedding.shape
    rows_total = rows_here * groups * pairs
    capacity = 2 * rows_here // groups
    slot_count = groups * capacity
    values = embedding.astype(jnp.float32)
    squares = jnp.sum(values * values, axis=1, keepdims=True)
    shifted = squares + 1e-06
    unit_rows = (values * lax.rsqrt(shifted)).astype(jnp.bfloat16)
    owner_group = labels // CL_OWN
    onehot = (owner_group[:, None] == jnp.arange(groups, dtype=jnp.int32)[None, :]).astype(
        jnp.int32
    )
    before = jnp.cumsum(onehot, axis=0) - onehot
    slot_index = owner_group * capacity + jnp.sum(before * onehot, axis=1)
    meta_column = lax.broadcasted_iota(jnp.int32, (rows_here, META), 1)
    meta = jnp.where(meta_column == 0, labels[:, None] + 1, 0)
    meta = jnp.where(meta_column == 1, order_ids[:, None] // 256, meta)
    meta = jnp.where(meta_column == 2, order_ids[:, None] % 256, meta).astype(jnp.bfloat16)
    packed = jnp.concatenate([unit_rows, meta], axis=1)
    send_rows = jnp.zeros((slot_count, width + META), jnp.bfloat16).at[slot_index].set(packed)
    got_rows = lax.all_to_all(
        send_rows.reshape(groups, capacity, -1), "dp", split_axis=0, concat_axis=0, tiled=True
    ).reshape(slot_count, -1)
    best_seen = pair_best(to_block(got_rows, width), slot_count, rows_total, pairs)
    lanes = jnp.pad(best_seen.reshape(groups, capacity), ((0, 0), (0, LANES - capacity)))
    answered = lax.all_to_all(lanes, "dp", split_axis=0, concat_axis=0, tiled=True)
    answered = answered[:, :capacity].reshape(1, slot_count)
    mine = slot_index[:, None] == jnp.arange(slot_count, dtype=jnp.int32)[None, :]
    return jnp.max(jnp.where(mine, answered, -jnp.inf), axis=1)


def solution(mesh):
    in_specs = (P(("dp", "pair"), None), P(("dp", "pair")), P(("dp", "pair")))
    out_specs = P(("dp", "pair"))
    return jax.shard_map(
        on_device, mesh=mesh, in_specs=in_specs, out_specs=out_specs, check_vma=False
    )
```

```python
import functools

import jax
import jax.numpy as jnp
from jax import lax
from jax.sharding import PartitionSpec as P

CL_OWN = 2
META = 128
LANES = 128
META_ROWS = 16


def tile_best(own_rows, own_key, other_rows, other_key, rows_total):
    scores = jnp.dot(own_rows, other_rows.T, preferred_element_type=jnp.float32)
    same_cluster = (other_key[None, :] // rows_total) == (own_key[:, None] // rows_total)
    earlier = same_cluster & (other_key[None, :] < own_key[:, None])
    return jnp.max(jnp.where(earlier, scores, -1.0), axis=1)


def to_block(got, width):
    slots = got.shape[0]
    meta = got[:, width : width + 3].T
    meta = jnp.pad(meta, ((0, META_ROWS - 3), (0, width - slots)))
    return jnp.concatenate([got[:, :width], meta], axis=0)


def block_best(query_block, key_block, slots, rows_total):
    query_key = block_keys(query_block, slots, rows_total)
    key_key = block_keys(key_block, slots, rows_total)
    return tile_best(query_block[:slots], query_key, key_block[:slots], key_key, rows_total)


def block_keys(block, slots, rows_total):
    meta = block[slots : slots + 3, :slots].astype(jnp.int32)
    return meta[0] * rows_total + meta[1] * 256 + meta[2]


def pair_best(block, slots, rows_total, pairs):
    chips = pairs // 2
    if pairs % 2 or chips != 4:
        gathered = lax.all_gather(block, "pair", axis=0, tiled=False)
        found = [block_best(block, gathered[i], slots, rows_total) for i in range(pairs)]
        return functools.reduce(jnp.maximum, found)

    def at(y, c):
        return (y % chips) * 2 + c

    def perm(to):
        return [(p, to(p // 2, p % 2)) for p in range(pairs)]

    swap = perm(lambda y, c: at(y, 1 - c))
    up = perm(lambda y, c: at(y + 1, c))
    down = perm(lambda y, c: at(y - 1, c))
    rows = block.shape[0]
    from_below = lax.ppermute(block, "pair", up)
    from_above = lax.ppermute(block, "pair", down)
    sibling_above = lax.ppermute(from_above, "pair", swap)

    def best_over(query, keys):
        found = [block_best(query, k, slots, rows_total) for k in keys]
        return functools.reduce(jnp.maximum, found)

    swapped = lax.ppermute(jnp.concatenate([block, from_below]), "pair", swap)
    sibling, sibling_below = swapped[:rows], swapped[rows:]
    for_below = best_over(from_below, [from_above, sibling_above])
    from_chip_above = lax.ppermute(for_below, "pair", down)
    sibling, sibling_below, _ = lax.optimization_barrier((sibling, sibling_below, for_below))
    best = best_over(
        block, [block, from_below, from_above, sibling, sibling_above, sibling_below]
    )
    return jnp.maximum(best, from_chip_above)


def on_device(embedding, labels, order_ids):
    groups = lax.axis_size("dp")
    pairs = lax.axis_size("pair")
    rows_here, width = embedding.shape
    rows_total = rows_here * groups * pairs
    capacity = 2 * rows_here // groups
    slot_count = groups * capacity
    values = embedding.astype(jnp.float32)
    squares = jnp.sum(values * values, axis=1, keepdims=True)
    shifted = squares + 1e-06
    unit_rows = (values * lax.rsqrt(shifted)).astype(jnp.bfloat16)
    owner_group = labels // CL_OWN
    onehot = (owner_group[:, None] == jnp.arange(groups, dtype=jnp.int32)[None, :]).astype(
        jnp.int32
    )
    before = jnp.cumsum(onehot, axis=0) - onehot
    slot_index = owner_group * capacity + jnp.sum(before * onehot, axis=1)
    meta_column = lax.broadcasted_iota(jnp.int32, (rows_here, META), 1)
    meta = jnp.where(meta_column == 0, labels[:, None] + 1, 0)
    meta = jnp.where(meta_column == 1, order_ids[:, None] // 256, meta)
    meta = jnp.where(meta_column == 2, order_ids[:, None] % 256, meta).astype(jnp.bfloat16)
    packed = jnp.concatenate([unit_rows, meta], axis=1)
    send_rows = jnp.zeros((slot_count, width + META), jnp.bfloat16).at[slot_index].set(packed)
    got_rows = lax.all_to_all(
        send_rows.reshape(groups, capacity, -1), "dp", split_axis=0, concat_axis=0, tiled=True
    ).reshape(slot_count, -1)
    best_seen = pair_best(to_block(got_rows, width), slot_count, rows_total, pairs)
    lanes = jnp.pad(best_seen.reshape(groups, capacity), ((0, 0), (0, LANES - capacity)))
    answered = lax.all_to_all(lanes, "dp", split_axis=0, concat_axis=0, tiled=True)
    answered = answered[:, :capacity].reshape(1, slot_count)
    mine = slot_index[:, None] == jnp.arange(slot_count, dtype=jnp.int32)[None, :]
    return jnp.max(jnp.where(mine, answered, -jnp.inf), axis=1)


def solution(mesh):
    in_specs = (P(("dp", "pair"), None), P(("dp", "pair")), P(("dp", "pair")))
    out_specs = P(("dp", "pair"))
    return jax.shard_map(
        on_device, mesh=mesh, in_specs=in_specs, out_specs=out_specs, check_vma=False
    )
```

```python
import functools

import jax
import jax.numpy as jnp
from jax import lax
from jax.sharding import PartitionSpec as P

CL_OWN = 2
META = 128
LANES = 128
META_ROWS = 16


def tile_best(own_rows, own_key, other_rows, other_key, rows_total):
    scores = jnp.dot(own_rows, other_rows.T, preferred_element_type=jnp.float32)
    same_cluster = (other_key[None, :] // rows_total) == (own_key[:, None] // rows_total)
    earlier = same_cluster & (other_key[None, :] < own_key[:, None])
    return jnp.max(jnp.where(earlier, scores, -1.0), axis=1)


def to_block(got, width):
    slots = got.shape[0]
    meta = got[:, width : width + 3].T
    meta = jnp.pad(meta, ((0, META_ROWS - 3), (0, width - slots)))
    return jnp.concatenate([got[:, :width], meta], axis=0)


def block_best(query_block, key_block, slots, rows_total):
    query_key = block_keys(query_block, slots, rows_total)
    key_key = block_keys(key_block, slots, rows_total)
    return tile_best(query_block[:slots], query_key, key_block[:slots], key_key, rows_total)


def block_keys(block, slots, rows_total):
    meta = block[slots : slots + 3, :slots].astype(jnp.int32)
    return meta[0] * rows_total + meta[1] * 256 + meta[2]


def pair_best(block, slots, rows_total, pairs):
    chips = pairs // 2
    if pairs % 2 or chips != 4:
        gathered = lax.all_gather(block, "pair", axis=0, tiled=False)
        found = [block_best(block, gathered[i], slots, rows_total) for i in range(pairs)]
        return functools.reduce(jnp.maximum, found)

    def at(y, c):
        return (y % chips) * 2 + c

    def perm(to):
        return [(p, to(p // 2, p % 2)) for p in range(pairs)]

    swap = perm(lambda y, c: at(y, 1 - c))
    up = perm(lambda y, c: at(y + 1, c))
    down = perm(lambda y, c: at(y - 1, c))
    rows = block.shape[0]
    from_below = lax.ppermute(block, "pair", up)
    from_above = lax.ppermute(block, "pair", down)
    swapped = lax.ppermute(jnp.concatenate([block, from_above]), "pair", swap)
    sibling, sibling_above = swapped[:rows], swapped[rows:]

    def best_over(query, keys):
        found = [block_best(query, k, slots, rows_total) for k in keys]
        return functools.reduce(jnp.maximum, found)

    for_below = best_over(from_below, [from_above, sibling_above])
    from_chip_above = lax.ppermute(for_below, "pair", down)
    later_below, _ = lax.optimization_barrier((from_below, for_below))
    sibling_below = lax.ppermute(later_below, "pair", swap)
    sibling, _ = lax.optimization_barrier((sibling, for_below))
    best = best_over(
        block, [block, from_below, from_above, sibling, sibling_above, sibling_below]
    )
    return jnp.maximum(best, from_chip_above)


def on_device(embedding, labels, order_ids):
    groups = lax.axis_size("dp")
    pairs = lax.axis_size("pair")
    rows_here, width = embedding.shape
    rows_total = rows_here * groups * pairs
    capacity = 2 * rows_here // groups
    slot_count = groups * capacity
    values = embedding.astype(jnp.float32)
    squares = jnp.sum(values * values, axis=1, keepdims=True)
    shifted = squares + 1e-06
    unit_rows = (values * lax.rsqrt(shifted)).astype(jnp.bfloat16)
    owner_group = labels // CL_OWN
    onehot = (owner_group[:, None] == jnp.arange(groups, dtype=jnp.int32)[None, :]).astype(
        jnp.int32
    )
    before = jnp.cumsum(onehot, axis=0) - onehot
    slot_index = owner_group * capacity + jnp.sum(before * onehot, axis=1)
    meta_column = lax.broadcasted_iota(jnp.int32, (rows_here, META), 1)
    meta = jnp.where(meta_column == 0, labels[:, None] + 1, 0)
    meta = jnp.where(meta_column == 1, order_ids[:, None] // 256, meta)
    meta = jnp.where(meta_column == 2, order_ids[:, None] % 256, meta).astype(jnp.bfloat16)
    packed = jnp.concatenate([unit_rows, meta], axis=1)
    send_rows = jnp.zeros((slot_count, width + META), jnp.bfloat16).at[slot_index].set(packed)
    got_rows = lax.all_to_all(
        send_rows.reshape(groups, capacity, -1), "dp", split_axis=0, concat_axis=0, tiled=True
    ).reshape(slot_count, -1)
    best_seen = pair_best(to_block(got_rows, width), slot_count, rows_total, pairs)
    lanes = jnp.pad(best_seen.reshape(groups, capacity), ((0, 0), (0, LANES - capacity)))
    answered = lax.all_to_all(lanes, "dp", split_axis=0, concat_axis=0, tiled=True)
    answered = answered[:, :capacity].reshape(1, slot_count)
    mine = slot_index[:, None] == jnp.arange(slot_count, dtype=jnp.int32)[None, :]
    return jnp.max(jnp.where(mine, answered, -jnp.inf), axis=1)


def solution(mesh):
    in_specs = (P(("dp", "pair"), None), P(("dp", "pair")), P(("dp", "pair")))
    out_specs = P(("dp", "pair"))
    return jax.shard_map(
        on_device, mesh=mesh, in_specs=in_specs, out_specs=out_specs, check_vma=False
    )
```

```python
import functools

import jax
import jax.numpy as jnp
from jax import lax
from jax.sharding import PartitionSpec as P

CL_OWN = 2
META = 128
LANES = 128
META_ROWS = 16


def tile_best(own_rows, own_key, other_rows, other_key, rows_total):
    scores = jnp.dot(own_rows, other_rows.T, preferred_element_type=jnp.float32)
    same_cluster = (other_key[None, :] // rows_total) == (own_key[:, None] // rows_total)
    earlier = same_cluster & (other_key[None, :] < own_key[:, None])
    return jnp.max(jnp.where(earlier, scores, -1.0), axis=1)


def to_block(got, width):
    slots = got.shape[0]
    meta = got[:, width : width + 3].T
    meta = jnp.pad(meta, ((0, META_ROWS - 3), (0, width - slots)))
    return jnp.concatenate([got[:, :width], meta], axis=0)


def block_best(query_block, key_block, slots, rows_total):
    query_key = block_keys(query_block, slots, rows_total)
    key_key = block_keys(key_block, slots, rows_total)
    return tile_best(query_block[:slots], query_key, key_block[:slots], key_key, rows_total)


def block_keys(block, slots, rows_total):
    meta = block[slots : slots + 3, :slots].astype(jnp.int32)
    return meta[0] * rows_total + meta[1] * 256 + meta[2]


def pair_best(block, slots, rows_total, pairs):
    chips = pairs // 2
    if pairs % 2 or chips != 4:
        gathered = lax.all_gather(block, "pair", axis=0, tiled=False)
        found = [block_best(block, gathered[i], slots, rows_total) for i in range(pairs)]
        return functools.reduce(jnp.maximum, found)

    def at(y, c):
        return (y % chips) * 2 + c

    def perm(to):
        return [(p, to(p // 2, p % 2)) for p in range(pairs)]

    swap = perm(lambda y, c: at(y, 1 - c))
    up = perm(lambda y, c: at(y + 1, c))
    down = perm(lambda y, c: at(y - 1, c))
    rows = block.shape[0]
    from_below = lax.ppermute(block, "pair", up)
    from_above = lax.ppermute(block, "pair", down)
    swapped = lax.ppermute(jnp.concatenate([block, from_above]), "pair", swap)
    sibling, sibling_above = swapped[:rows], swapped[rows:]

    def best_over(query, keys):
        found = [block_best(query, k, slots, rows_total) for k in keys]
        return functools.reduce(jnp.maximum, found)

    sibling_below = lax.ppermute(from_below, "pair", swap)
    for_below = best_over(from_below, [from_above, sibling_above])
    from_chip_above = lax.ppermute(for_below, "pair", down)
    late = lax.optimization_barrier(
        (block, from_below, from_above, sibling, sibling_above, sibling_below, for_below)
    )
    best = best_over(late[0], list(late[:6]))
    return jnp.maximum(best, from_chip_above)


def on_device(embedding, labels, order_ids):
    groups = lax.axis_size("dp")
    pairs = lax.axis_size("pair")
    rows_here, width = embedding.shape
    rows_total = rows_here * groups * pairs
    capacity = 2 * rows_here // groups
    slot_count = groups * capacity
    values = embedding.astype(jnp.float32)
    squares = jnp.sum(values * values, axis=1, keepdims=True)
    shifted = squares + 1e-06
    unit_rows = (values * lax.rsqrt(shifted)).astype(jnp.bfloat16)
    owner_group = labels // CL_OWN
    onehot = (owner_group[:, None] == jnp.arange(groups, dtype=jnp.int32)[None, :]).astype(
        jnp.int32
    )
    before = jnp.cumsum(onehot, axis=0) - onehot
    slot_index = owner_group * capacity + jnp.sum(before * onehot, axis=1)
    meta_column = lax.broadcasted_iota(jnp.int32, (rows_here, META), 1)
    meta = jnp.where(meta_column == 0, labels[:, None] + 1, 0)
    meta = jnp.where(meta_column == 1, order_ids[:, None] // 256, meta)
    meta = jnp.where(meta_column == 2, order_ids[:, None] % 256, meta).astype(jnp.bfloat16)
    packed = jnp.concatenate([unit_rows, meta], axis=1)
    send_rows = jnp.zeros((slot_count, width + META), jnp.bfloat16).at[slot_index].set(packed)
    got_rows = lax.all_to_all(
        send_rows.reshape(groups, capacity, -1), "dp", split_axis=0, concat_axis=0, tiled=True
    ).reshape(slot_count, -1)
    best_seen = pair_best(to_block(got_rows, width), slot_count, rows_total, pairs)
    lanes = jnp.pad(best_seen.reshape(groups, capacity), ((0, 0), (0, LANES - capacity)))
    answered = lax.all_to_all(lanes, "dp", split_axis=0, concat_axis=0, tiled=True)
    answered = answered[:, :capacity].reshape(1, slot_count)
    mine = slot_index[:, None] == jnp.arange(slot_count, dtype=jnp.int32)[None, :]
    return jnp.max(jnp.where(mine, answered, -jnp.inf), axis=1)


def solution(mesh):
    in_specs = (P(("dp", "pair"), None), P(("dp", "pair")), P(("dp", "pair")))
    out_specs = P(("dp", "pair"))
    return jax.shard_map(
        on_device, mesh=mesh, in_specs=in_specs, out_specs=out_specs, check_vma=False
    )
```

```python
import functools

import jax
import jax.numpy as jnp
from jax import lax
from jax.sharding import PartitionSpec as P

CL_OWN = 2
META = 128
LANES = 128
META_ROWS = 16


def tile_best(own_rows, own_key, other_rows, other_key, rows_total):
    scores = jnp.dot(own_rows, other_rows.T, preferred_element_type=jnp.float32)
    same_cluster = (other_key[None, :] // rows_total) == (own_key[:, None] // rows_total)
    earlier = same_cluster & (other_key[None, :] < own_key[:, None])
    return jnp.max(jnp.where(earlier, scores, -1.0), axis=1)


def to_block(got, width):
    slots = got.shape[0]
    meta = got[:, width : width + 3].T
    meta = jnp.pad(meta, ((0, META_ROWS - 3), (0, width - slots)))
    return jnp.concatenate([got[:, :width], meta], axis=0)


def block_best(query_block, key_block, slots, rows_total):
    query_key = block_keys(query_block, slots, rows_total)
    key_key = block_keys(key_block, slots, rows_total)
    return tile_best(query_block[:slots], query_key, key_block[:slots], key_key, rows_total)


def block_keys(block, slots, rows_total):
    meta = block[slots : slots + 3, :slots].astype(jnp.int32)
    return meta[0] * rows_total + meta[1] * 256 + meta[2]


def pair_best(block, slots, rows_total, pairs):
    chips = pairs // 2
    if pairs % 2 or chips != 4:
        gathered = lax.all_gather(block, "pair", axis=0, tiled=False)
        found = [block_best(block, gathered[i], slots, rows_total) for i in range(pairs)]
        return functools.reduce(jnp.maximum, found)

    def at(y, c):
        return (y % chips) * 2 + c

    def perm(to):
        return [(p, to(p // 2, p % 2)) for p in range(pairs)]

    swap = perm(lambda y, c: at(y, 1 - c))
    up = perm(lambda y, c: at(y + 1, c))
    down = perm(lambda y, c: at(y - 1, c))
    rows = block.shape[0]
    from_below = lax.ppermute(block, "pair", up)
    from_above = lax.ppermute(block, "pair", down)
    swapped = lax.ppermute(jnp.concatenate([block, from_above]), "pair", swap)
    sibling, sibling_above = swapped[:rows], swapped[rows:]

    def best_over(query, keys):
        found = [block_best(query, k, slots, rows_total) for k in keys]
        return functools.reduce(jnp.maximum, found)

    for_below = best_over(from_below, [from_above, sibling_above])
    from_chip_above = lax.ppermute(for_below, "pair", down)
    later_below, _ = lax.optimization_barrier((from_below, for_below))
    sibling_below = lax.ppermute(later_below, "pair", swap)
    late = lax.optimization_barrier(
        (block, from_below, from_above, sibling, sibling_above, sibling_below, for_below)
    )
    best = best_over(late[0], list(late[:6]))
    return jnp.maximum(best, from_chip_above)


def on_device(embedding, labels, order_ids):
    groups = lax.axis_size("dp")
    pairs = lax.axis_size("pair")
    rows_here, width = embedding.shape
    rows_total = rows_here * groups * pairs
    capacity = 2 * rows_here // groups
    slot_count = groups * capacity
    values = embedding.astype(jnp.float32)
    squares = jnp.sum(values * values, axis=1, keepdims=True)
    shifted = squares + 1e-06
    unit_rows = (values * lax.rsqrt(shifted)).astype(jnp.bfloat16)
    owner_group = labels // CL_OWN
    onehot = (owner_group[:, None] == jnp.arange(groups, dtype=jnp.int32)[None, :]).astype(
        jnp.int32
    )
    before = jnp.cumsum(onehot, axis=0) - onehot
    slot_index = owner_group * capacity + jnp.sum(before * onehot, axis=1)
    meta_column = lax.broadcasted_iota(jnp.int32, (rows_here, META), 1)
    meta = jnp.where(meta_column == 0, labels[:, None] + 1, 0)
    meta = jnp.where(meta_column == 1, order_ids[:, None] // 256, meta)
    meta = jnp.where(meta_column == 2, order_ids[:, None] % 256, meta).astype(jnp.bfloat16)
    packed = jnp.concatenate([unit_rows, meta], axis=1)
    send_rows = jnp.zeros((slot_count, width + META), jnp.bfloat16).at[slot_index].set(packed)
    got_rows = lax.all_to_all(
        send_rows.reshape(groups, capacity, -1), "dp", split_axis=0, concat_axis=0, tiled=True
    ).reshape(slot_count, -1)
    best_seen = pair_best(to_block(got_rows, width), slot_count, rows_total, pairs)
    lanes = jnp.pad(best_seen.reshape(groups, capacity), ((0, 0), (0, LANES - capacity)))
    answered = lax.all_to_all(lanes, "dp", split_axis=0, concat_axis=0, tiled=True)
    answered = answered[:, :capacity].reshape(1, slot_count)
    mine = slot_index[:, None] == jnp.arange(slot_count, dtype=jnp.int32)[None, :]
    return jnp.max(jnp.where(mine, answered, -jnp.inf), axis=1)


def solution(mesh):
    in_specs = (P(("dp", "pair"), None), P(("dp", "pair")), P(("dp", "pair")))
    out_specs = P(("dp", "pair"))
    return jax.shard_map(
        on_device, mesh=mesh, in_specs=in_specs, out_specs=out_specs, check_vma=False
    )
```

```python
import functools

import jax
import jax.numpy as jnp
from jax import lax
from jax.sharding import PartitionSpec as P

CL_OWN = 2
META = 128
LANES = 128
META_ROWS = 16


def tile_best(own_rows, own_key, other_rows, other_key, rows_total):
    scores = jnp.dot(own_rows, other_rows.T, preferred_element_type=jnp.float32)
    same_cluster = (other_key[None, :] // rows_total) == (own_key[:, None] // rows_total)
    earlier = same_cluster & (other_key[None, :] < own_key[:, None])
    return jnp.max(jnp.where(earlier, scores, -1.0), axis=1)


def to_block(got, width):
    slots = got.shape[0]
    meta = got[:, width : width + 3].T
    meta = jnp.pad(meta, ((0, META_ROWS - 3), (0, width - slots)))
    return jnp.concatenate([got[:, :width], meta], axis=0)


def block_best(query_block, key_block, slots, rows_total):
    query_key = block_keys(query_block, slots, rows_total)
    key_key = block_keys(key_block, slots, rows_total)
    return tile_best(query_block[:slots], query_key, key_block[:slots], key_key, rows_total)


def block_keys(block, slots, rows_total):
    meta = block[slots : slots + 3, :slots].astype(jnp.int32)
    return meta[0] * rows_total + meta[1] * 256 + meta[2]


def pair_best(block, slots, rows_total, pairs):
    chips = pairs // 2
    if pairs % 2 or chips != 4:
        gathered = lax.all_gather(block, "pair", axis=0, tiled=False)
        found = [block_best(block, gathered[i], slots, rows_total) for i in range(pairs)]
        return functools.reduce(jnp.maximum, found)

    def at(y, c):
        return (y % chips) * 2 + c

    def perm(to):
        return [(p, to(p // 2, p % 2)) for p in range(pairs)]

    swap = perm(lambda y, c: at(y, 1 - c))
    up = perm(lambda y, c: at(y + 1, c))
    down = perm(lambda y, c: at(y - 1, c))
    rows = block.shape[0]
    from_below = lax.ppermute(block, "pair", up)
    from_above = lax.ppermute(block, "pair", down)
    sibling_above = lax.ppermute(from_above, "pair", swap)

    def best_over(query, keys):
        found = [block_best(query, k, slots, rows_total) for k in keys]
        return functools.reduce(jnp.maximum, found)

    swapped = lax.ppermute(jnp.concatenate([block, from_below]), "pair", swap)
    sibling, sibling_below = swapped[:rows], swapped[rows:]
    for_below = best_over(from_below, [from_above, sibling_above])
    from_chip_above = lax.ppermute(for_below, "pair", down)
    late = lax.optimization_barrier(
        (block, from_below, from_above, sibling, sibling_above, sibling_below, for_below)
    )
    best = best_over(late[0], list(late[:6]))
    return jnp.maximum(best, from_chip_above)


def on_device(embedding, labels, order_ids):
    groups = lax.axis_size("dp")
    pairs = lax.axis_size("pair")
    rows_here, width = embedding.shape
    rows_total = rows_here * groups * pairs
    capacity = 2 * rows_here // groups
    slot_count = groups * capacity
    values = embedding.astype(jnp.float32)
    squares = jnp.sum(values * values, axis=1, keepdims=True)
    shifted = squares + 1e-06
    unit_rows = (values * lax.rsqrt(shifted)).astype(jnp.bfloat16)
    owner_group = labels // CL_OWN
    onehot = (owner_group[:, None] == jnp.arange(groups, dtype=jnp.int32)[None, :]).astype(
        jnp.int32
    )
    before = jnp.cumsum(onehot, axis=0) - onehot
    slot_index = owner_group * capacity + jnp.sum(before * onehot, axis=1)
    meta_column = lax.broadcasted_iota(jnp.int32, (rows_here, META), 1)
    meta = jnp.where(meta_column == 0, labels[:, None] + 1, 0)
    meta = jnp.where(meta_column == 1, order_ids[:, None] // 256, meta)
    meta = jnp.where(meta_column == 2, order_ids[:, None] % 256, meta).astype(jnp.bfloat16)
    packed = jnp.concatenate([unit_rows, meta], axis=1)
    send_rows = jnp.zeros((slot_count, width + META), jnp.bfloat16).at[slot_index].set(packed)
    got_rows = lax.all_to_all(
        send_rows.reshape(groups, capacity, -1), "dp", split_axis=0, concat_axis=0, tiled=True
    ).reshape(slot_count, -1)
    best_seen = pair_best(to_block(got_rows, width), slot_count, rows_total, pairs)
    lanes = jnp.pad(best_seen.reshape(groups, capacity), ((0, 0), (0, LANES - capacity)))
    answered = lax.all_to_all(lanes, "dp", split_axis=0, concat_axis=0, tiled=True)
    answered = answered[:, :capacity].reshape(1, slot_count)
    mine = slot_index[:, None] == jnp.arange(slot_count, dtype=jnp.int32)[None, :]
    return jnp.max(jnp.where(mine, answered, -jnp.inf), axis=1)


def solution(mesh):
    in_specs = (P(("dp", "pair"), None), P(("dp", "pair")), P(("dp", "pair")))
    out_specs = P(("dp", "pair"))
    return jax.shard_map(
        on_device, mesh=mesh, in_specs=in_specs, out_specs=out_specs, check_vma=False
    )
```
